256 devices in a mesh: ctx: 64 (over z, x, y_lo), tp: 4 (over y_hi, core).
Axes of the slice: x: 4, y: 4 (y_hi: 2, y_lo: 2; y = y_hi * 2 + y_lo), z: 8, core: 2. Of those that a mesh axis runs over, the one named last changes fastest.
Arguments:
- query_rows: bfloat16 [32768, 2048], P('ctx', 'tp'), may hold values from -5 to 5
- key_rows: bfloat16 [32768, 512], P('ctx', 'tp'), may hold values from -5 to 5
- value_rows: bfloat16 [32768, 512], P('ctx', 'tp'), may hold values from -6 to 6
- out_weight: bfloat16 [2048, 4096], P('tp'), may hold values from -0.125 to 0.125
- out_grad: bfloat16 [32768, 4096], P(('ctx', 'tp')), may hold values from -24 to 24
- doc_ids: int32 [32768], replicated, may hold values from 0 to 7, never falling along the last dimension, each value on 1 to 16384 neighbouring positions
- window_blocks: int32 [256], replicated, may hold values from 1 to 12, as said below
Outputs:
- layer_out: bfloat16 [32768, 4096], P(('ctx', 'tp'))
- grad_queries: bfloat16 [32768, 2048], P('ctx', 'tp')
- grad_keys: bfloat16 [32768, 512], P('ctx', 'tp')
- grad_values: bfloat16 [32768, 512], P('ctx', 'tp')
- grad_weight: float32 [2048, 4096], P('tp', 'ctx')
The draws below stay inside these ranges and needn't reach their ends.
Inputs may be any that keep to these rules, and one draw needn't show every extreme that they name: `window_blocks`: some query block has the full window of 12 blocks.
All inputs are finite; a program needn't handle non-finite values.
Results may differ from the reference program's by a relative error of at most 0.019.
Values may be sent and summed in bfloat16 or wider, within the bound.
No kernel may reach another device: no remote copies, remote signals or barrier semaphores. Data moves between devices by JAX's collectives and lax.ppermute only.
A program may use at most 128 MiB of HBM per device.

```python
import math
import jax
import jax.numpy as jnp
import numpy as np
from jax import lax

D = 4096
HEADS = 16
KV_HEADS = 4
HEAD_DIM = 128
BLOCK = 128
WINDOW_BLOCKS = 12
SEQ = 32768
NBLOCKS = 256
DOCS = 8


def draw_query_rows(key, part):
    base = jnp.clip(jax.random.normal(jax.random.fold_in(key, 21), (SEQ, HEADS * HEAD_DIM)), -5.0, 5.0)
    return base.astype(jnp.bfloat16)


def draw_key_rows(key, part):
    base = jnp.clip(jax.random.normal(jax.random.fold_in(key, 22), (SEQ, KV_HEADS * HEAD_DIM)), -5.0, 5.0)
    return base.astype(jnp.bfloat16)


def draw_window_blocks(key, part):
    widths = jax.random.randint(jax.random.fold_in(key, 31), (NBLOCKS,), 1, WINDOW_BLOCKS + 1)
    where_full = jax.random.randint(jax.random.fold_in(key, 32), (), 0, NBLOCKS)
    where_one = (where_full + NBLOCKS // 2) % NBLOCKS
    widths = widths.at[where_full].set(WINDOW_BLOCKS).at[where_one].set(1)
    return widths.astype(jnp.int32)


def raised(array, stream_key, source, target, parts, factor):
    def block_of(axis_at):
        return (jnp.arange(array.shape[axis_at]) // (array.shape[axis_at] // parts)).reshape((-1,) + (1,) * (array.ndim - 1 - axis_at))

    one_side = jax.random.permutation(stream_key, parts)[block_of(target)]
    other_side = (block_of(target) + parts // 2) % parts
    return jnp.where((block_of(source) == one_side) | (block_of(source) == other_side), factor * array, array)


def steps_of(key, extent, split, low, high):
    level, own = 1.0, jax.random.fold_in(key, 6)
    for dim, blocks in split:
        heights = jnp.exp(jax.random.uniform(jax.random.fold_in(own, dim), (blocks,), jnp.float32, low / len(split), high / len(split)))
        level = level * jnp.repeat(heights, extent[dim] // blocks).reshape([-1 if axis == dim else 1 for axis in range(len(extent))])
    return level


def profile(number_of, total, reach, lean):
    weights = [(1 << 20) // math.isqrt(rank ** lean) + 1 for rank in range(2, number_of + 1)]
    surplus, given = total - reach - (number_of - 1), [1] * (number_of - 1)
    while surplus > 0:
        movable = [i for i in range(number_of - 1) if given[i] < reach]
        whole, remaining = sum([weights[i] for i in movable]), surplus
        for i in movable:
            more = min(reach - given[i], max(1, remaining * weights[i] // whole), surplus)
            given[i] = given[i] + more
            surplus = surplus - more
    return np.array([reach] + given)


def uneven(own_key, amount, total, limit, lean):
    if amount == 2:
        one = jax.random.randint(own_key, (), max(1, total - limit), min(limit, total - 1) + 1)
        return jnp.stack([one, total - one])
    sizes = jnp.asarray(profile(amount, total, limit, lean), jnp.int32)
    pairs = (amount - 1) // 2
    source_of, sink = sizes[1:1 + 2 * pairs:2], sizes[2:2 + 2 * pairs:2]
    margin = jnp.minimum(source_of - 1, limit - sink)
    moved = jax.random.randint(jax.random.fold_in(own_key, 1), (pairs,), 0, 1 << 20) % (margin + 1)
    sizes = sizes.at[1:1 + 2 * pairs:2].set(source_of - moved).at[2:2 + 2 * pairs:2].set(sink + moved)
    return sizes[jax.random.permutation(jax.random.fold_in(own_key, 2), amount)]


def bell_draw(stream_key, shape, scale, reach, split=(), held_as=jnp.bfloat16):
    result = scale * jax.random.normal(stream_key, shape, jnp.float32)
    if split:
        result = result * steps_of(stream_key, shape, split, -0.22, 0.18)
    return jnp.clip(result, -reach, reach).astype(held_as)


def noise_with(stream_key, shape, scale, limit, split, heavy, held_as=jnp.bfloat16):
    values = scale * jax.random.normal(stream_key, shape, jnp.float32)
    if split:
        values = values * steps_of(stream_key, shape, split, -0.22, 0.18)
    return jnp.clip(raised(values, jax.random.fold_in(stream_key, 3), *heavy), -limit, limit).astype(held_as)


def setup_inputs(seed: int = 0) -> dict:
    keys = jax.random.split(jax.random.key(seed), 8)
    query_rows = draw_query_rows(jax.random.fold_in(keys[7], 71), 0)
    key_rows = draw_key_rows(jax.random.fold_in(keys[7], 71), 0)
    value_rows = bell_draw(keys[2], (SEQ, KV_HEADS * HEAD_DIM), 1.0, 6.0, ((0, 64), (1, 4)))
    out_weight = bell_draw(keys[3], (HEADS * HEAD_DIM, D), (HEADS * HEAD_DIM) ** -0.5, 0.125, ((0, 4),))
    out_grad = noise_with(keys[4], (SEQ, D), 1.0, 24.0, ((0, 256),), (0, 1, 256, 6.0))
    doc_ids = jnp.searchsorted(jnp.cumsum(uneven(keys[5], DOCS, SEQ, SEQ // 2, 2)), jnp.arange(SEQ), side="right").astype(jnp.int32)
    window_blocks = draw_window_blocks(jax.random.fold_in(keys[7], 71), 0)
    return dict(query_rows=query_rows, key_rows=key_rows, value_rows=value_rows, out_weight=out_weight, out_grad=out_grad, doc_ids=doc_ids, window_blocks=window_blocks)


NEG_FILL = -1e30


def block_mask(doc_pad, window_blocks, block_index, span):
    query_pos = block_index * BLOCK + jnp.arange(BLOCK, dtype=jnp.int32)
    key_pos = block_index * BLOCK - span + jnp.arange(span + BLOCK, dtype=jnp.int32)
    query_doc = lax.dynamic_slice_in_dim(doc_pad, span + block_index * BLOCK, BLOCK)
    key_doc = lax.dynamic_slice_in_dim(doc_pad, block_index * BLOCK, span + BLOCK)
    width_here = window_blocks[block_index]
    return ((key_pos[None, :] <= query_pos[:, None])
            & (query_doc[:, None] == key_doc[None, :])
            & (block_index - key_pos[None, :] // BLOCK < width_here))


def reference(query_rows, key_rows, value_rows, out_weight, out_grad, doc_ids, window_blocks):
    seq_len = query_rows.shape[0]
    groups = HEADS // KV_HEADS
    score_scale = HEAD_DIM ** -0.5
    span = (WINDOW_BLOCKS - 1) * BLOCK
    block_count = seq_len // BLOCK
    kv_width = KV_HEADS * HEAD_DIM
    key_pad = jnp.concatenate([jnp.zeros((span, kv_width), key_rows.dtype), key_rows], axis=0)
    value_pad = jnp.concatenate([jnp.zeros((span, kv_width), value_rows.dtype), value_rows], axis=0)
    doc_pad = jnp.concatenate([jnp.full((span,), -1, jnp.int32), doc_ids.astype(jnp.int32)])
    query_four = query_rows.reshape(block_count, BLOCK, KV_HEADS, groups, HEAD_DIM)

    def load_block(block_index):
        queries_here = query_four[block_index].astype(jnp.float32)
        keys_here = lax.dynamic_slice_in_dim(key_pad, block_index * BLOCK, span + BLOCK)
        keys_here = keys_here.reshape(span + BLOCK, KV_HEADS, HEAD_DIM).astype(jnp.float32)
        values_here = lax.dynamic_slice_in_dim(value_pad, block_index * BLOCK, span + BLOCK)
        values_here = values_here.reshape(span + BLOCK, KV_HEADS, HEAD_DIM).astype(jnp.float32)
        scores = jnp.einsum("qcgd,kcd->cgqk", queries_here, keys_here) * score_scale
        allowed = block_mask(doc_pad, window_blocks, block_index, span)
        return queries_here, keys_here, values_here, scores, allowed

    def forward_block(block_index):
        queries_here, keys_here, values_here, scores, allowed = load_block(block_index)
        masked = jnp.where(allowed, scores, NEG_FILL)
        row_max = jnp.max(masked, axis=-1)
        expo = jnp.where(allowed, jnp.exp(masked - row_max[..., None]), 0.0)
        total = jnp.sum(expo, axis=-1)
        expo_half = lax.optimization_barrier(expo.astype(jnp.bfloat16)).astype(jnp.float32)
        summed = jnp.einsum("cgqk,kcd->qcgd", expo_half, values_here)
        attn_here = (summed / jnp.transpose(total, (2, 0, 1))[..., None]).reshape(BLOCK, -1)
        return attn_here.astype(jnp.bfloat16), row_max + jnp.log(total)

    attn_blocks, lse_blocks = lax.map(forward_block, jnp.arange(block_count, dtype=jnp.int32))
    attn = attn_blocks.reshape(seq_len, HEADS * HEAD_DIM)
    layer_out = jnp.dot(attn, out_weight, preferred_element_type=jnp.float32).astype(jnp.bfloat16)
    d_attn = jnp.dot(out_grad, out_weight.T, preferred_element_type=jnp.float32).astype(jnp.bfloat16)
    grad_weight = jnp.dot(attn.T, out_grad, preferred_element_type=jnp.float32) * (seq_len ** -0.5)
    grad_four = d_attn.reshape(block_count, BLOCK, KV_HEADS, groups, HEAD_DIM)
    attn_four = attn.reshape(block_count, BLOCK, KV_HEADS, groups, HEAD_DIM)
    delta_all = jnp.sum(grad_four.astype(jnp.float32) * attn_four.astype(jnp.float32), axis=-1)

    def backward_block(carried, block_index):
        key_acc, value_acc = carried
        queries_here, keys_here, values_here, scores, allowed = load_block(block_index)
        lse_here = lse_blocks[block_index]
        probs = jnp.exp(jnp.where(allowed, scores - lse_here[..., None], NEG_FILL))
        grad_here = grad_four[block_index].astype(jnp.float32)
        delta_here = jnp.transpose(delta_all[block_index], (1, 2, 0))
        d_probs = jnp.einsum("qcgd,kcd->cgqk", grad_here, values_here)
        d_scores = (probs * (d_probs - delta_here[..., None]) * score_scale).astype(jnp.bfloat16)
        d_scores = lax.optimization_barrier(d_scores).astype(jnp.float32)
        probs_half = lax.optimization_barrier(probs.astype(jnp.bfloat16)).astype(jnp.float32)
        grad_q = jnp.einsum("cgqk,kcd->qcgd", d_scores, keys_here).reshape(BLOCK, -1).astype(jnp.bfloat16)
        grad_k = jnp.einsum("cgqk,qcgd->kcd", d_scores, queries_here).reshape(span + BLOCK, kv_width)
        grad_v = jnp.einsum("cgqk,qcgd->kcd", probs_half, grad_here).reshape(span + BLOCK, kv_width)
        start = block_index * BLOCK
        key_acc = lax.dynamic_update_slice_in_dim(
            key_acc, lax.dynamic_slice_in_dim(key_acc, start, span + BLOCK) + grad_k, start, 0)
        value_acc = lax.dynamic_update_slice_in_dim(
            value_acc, lax.dynamic_slice_in_dim(value_acc, start, span + BLOCK) + grad_v, start, 0)
        return (key_acc, value_acc), grad_q

    zeros_pad = jnp.zeros((seq_len + span, kv_width), jnp.float32)
    (key_acc, value_acc), grad_q_blocks = lax.scan(
        backward_block, (zeros_pad, zeros_pad), jnp.arange(block_count, dtype=jnp.int32))
    grad_queries = grad_q_blocks.reshape(seq_len, HEADS * HEAD_DIM)
    grad_keys = key_acc[span:].astype(jnp.bfloat16)
    grad_values = value_acc[span:].astype(jnp.bfloat16)
    return (layer_out, grad_queries, grad_keys, grad_values, grad_weight)
```

```python
import jax
import jax.numpy as jnp
import numpy as np
from jax import lax
from jax.sharding import Mesh
from jax.sharding import PartitionSpec as P

HEAD_DIM = 128
BLOCK = 128
REACH = 3
NEG_FILL = -1e30

CTX_PARTS = (("z", 8), ("x", 4), ("y_lo", 2))
TP_PARTS = (("y_hi", 2), ("core", 2))
CTX = tuple(name for name, _ in CTX_PARTS)
TP = tuple(name for name, _ in TP_PARTS)


def from_earlier(block, distance, count):
    route = [(i - distance, i) for i in range(count) if 0 <= i - distance < count]
    return lax.ppermute(block, CTX, route)


def to_earlier(block, distance, count):
    route = [(i, i - distance) for i in range(count) if 0 <= i - distance < count]
    return lax.ppermute(block, CTX, route)


def rotated(block, distance, count):
    route = [((i - distance) % count, i) for i in range(count)]
    return lax.ppermute(block, TP, route)


def on_device(query_rows, key_rows, value_rows, out_weight, out_grad, doc_ids, window_blocks):
    tokens_here = query_rows.shape[0]
    kv_width = key_rows.shape[1]
    kv_here = kv_width // HEAD_DIM
    groups = query_rows.shape[1] // kv_width
    score_scale = HEAD_DIM ** (-0.5)
    ctx_count = lax.axis_size(CTX)
    tp_count = lax.axis_size(TP)
    ctx_place = lax.axis_index(CTX)
    tp_place = lax.axis_index(TP)
    my_start = ctx_place * tokens_here
    span = REACH * tokens_here
    key_count = span + tokens_here

    grad_piece = lax.all_gather(out_grad, TP, axis=0, tiled=True)

    earlier = [
        from_earlier((key_rows, value_rows), distance, ctx_count)
        for distance in range(REACH, 0, -1)
    ]
    keys_all = jnp.concatenate([pair[0] for pair in earlier] + [key_rows], axis=0)
    values_all = jnp.concatenate([pair[1] for pair in earlier] + [value_rows], axis=0)
    key_heads = keys_all.reshape(key_count, kv_here, HEAD_DIM)
    value_heads = values_all.reshape(key_count, kv_here, HEAD_DIM)

    doc_pad = jnp.concatenate([jnp.full((span,), -1, jnp.int32), doc_ids.astype(jnp.int32)])
    query_pos = my_start + jnp.arange(tokens_here, dtype=jnp.int32)
    key_pos = my_start - span + jnp.arange(key_count, dtype=jnp.int32)
    query_doc = lax.dynamic_slice_in_dim(doc_ids, my_start, tokens_here)
    key_doc = lax.dynamic_slice_in_dim(doc_pad, my_start, key_count)
    query_width = jnp.repeat(
        lax.dynamic_slice_in_dim(window_blocks, my_start // BLOCK, tokens_here // BLOCK), BLOCK
    )
    allowed = (
        (key_pos[None, :] >= 0)
        & (key_pos[None, :] <= query_pos[:, None])
        & (query_doc[:, None] == key_doc[None, :])
        & (query_pos[:, None] // BLOCK - key_pos[None, :] // BLOCK < query_width[:, None])
    )

    query_four = query_rows.reshape(tokens_here, kv_here, groups, HEAD_DIM)
    scores = (
        jnp.einsum("qcgd,kcd->cgqk", query_four, key_heads, preferred_element_type=jnp.float32)
        * score_scale
    )
    masked = jnp.where(allowed, scores, NEG_FILL)
    row_max = jnp.max(masked, axis=-1)
    expo = jnp.where(allowed, jnp.exp(masked - row_max[..., None]), 0.0)
    total = jnp.sum(expo, axis=-1)
    summed = jnp.einsum(
        "cgqk,kcd->qcgd", expo.astype(jnp.bfloat16), value_heads, preferred_element_type=jnp.float32
    )
    attn_four = summed / jnp.transpose(total, (2, 0, 1))[..., None]
    attn = attn_four.reshape(tokens_here, -1).astype(jnp.bfloat16)
    log_sum = row_max + jnp.log(total)

    out_part = jnp.dot(attn, out_weight, preferred_element_type=jnp.float32)
    out_chunks = out_part.reshape(tp_count, tokens_here // tp_count, out_part.shape[1])
    layer_sum = lax.dynamic_index_in_dim(out_chunks, tp_place, 0, keepdims=False)
    for distance in range(1, tp_count):
        chunk = lax.dynamic_index_in_dim(
            out_chunks, (tp_place + distance) % tp_count, 0, keepdims=False
        )
        layer_sum = layer_sum + rotated(chunk.astype(jnp.bfloat16), distance, tp_count).astype(
            jnp.float32
        )
    layer_out = layer_sum.astype(jnp.bfloat16)

    weight_part = lax.dot_general(
        attn, grad_piece, (((0,), (0,)), ((), ())), preferred_element_type=jnp.float32
    )
    weight_sum = weight_part.astype(jnp.bfloat16)
    for stage, (name, _) in enumerate(CTX_PARTS):
        weight_sum = lax.psum_scatter(weight_sum, name, scatter_dimension=1, tiled=True)
        if stage == 0:
            weight_sum = weight_sum.astype(jnp.float32)
    seq_total = ctx_count * tokens_here
    grad_weight = weight_sum * seq_total ** (-0.5)

    d_attn = lax.dot_general(
        grad_piece, out_weight, (((1,), (1,)), ((), ())), preferred_element_type=jnp.float32
    ).astype(jnp.bfloat16)
    grad_four = d_attn.reshape(tokens_here, kv_here, groups, HEAD_DIM)
    delta_rows = jnp.transpose(
        jnp.sum(
            grad_four.astype(jnp.float32)
            * attn.reshape(tokens_here, kv_here, groups, HEAD_DIM).astype(jnp.float32),
            axis=-1,
        ),
        (1, 2, 0),
    )

    probs = jnp.exp(jnp.where(allowed, scores - log_sum[..., None], NEG_FILL))
    d_probs = jnp.einsum(
        "qcgd,kcd->cgqk", grad_four, value_heads, preferred_element_type=jnp.float32
    )
    d_scores = (probs * (d_probs - delta_rows[..., None]) * score_scale).astype(jnp.bfloat16)
    query_grad = jnp.einsum(
        "cgqk,kcd->qcgd", d_scores, key_heads, preferred_element_type=jnp.float32
    )
    key_grad_all = jnp.einsum(
        "cgqk,qcgd->kcd", d_scores, query_four, preferred_element_type=jnp.float32
    ).reshape(key_count, kv_width)
    value_grad_all = jnp.einsum(
        "cgqk,qcgd->kcd", probs.astype(jnp.bfloat16), grad_four, preferred_element_type=jnp.float32
    ).reshape(key_count, kv_width)

    key_grad = key_grad_all[span:]
    value_grad = value_grad_all[span:]
    for distance in range(1, REACH + 1):
        lo = span - distance * tokens_here
        sent = to_earlier(
            (
                key_grad_all[lo : lo + tokens_here].astype(jnp.bfloat16),
                value_grad_all[lo : lo + tokens_here].astype(jnp.bfloat16),
            ),
            distance,
            ctx_count,
        )
        key_grad = key_grad + sent[0].astype(jnp.float32)
        value_grad = value_grad + sent[1].astype(jnp.float32)

    grad_queries = query_grad.reshape(tokens_here, -1).astype(jnp.bfloat16)
    grad_keys = key_grad.astype(jnp.bfloat16)
    grad_values = value_grad.astype(jnp.bfloat16)
    return (layer_out, grad_queries, grad_keys, grad_values, grad_weight)


def solution(mesh):
    shape = tuple(size for _, size in CTX_PARTS + TP_PARTS)
    fine = Mesh(np.asarray(mesh.devices).reshape(shape), CTX + TP)
    placed = (
        P(CTX, TP),
        P(CTX, TP),
        P(CTX, TP),
        P(TP, None),
        P(CTX + TP, None),
        P(),
        P(),
    )
    return jax.shard_map(
        on_device,
        mesh=fine,
        in_specs=placed,
        out_specs=(
            P(CTX + TP, None),
            P(CTX, TP),
            P(CTX, TP),
            P(CTX, TP),
            P(TP, CTX),
        ),
        check_vma=False,
    )
```

```python
import jax
import jax.numpy as jnp
import numpy as np
from jax import lax
from jax.sharding import Mesh
from jax.sharding import PartitionSpec as P

HEAD_DIM = 128
BLOCK = 128
REACH = 3
NEG_FILL = -1e30

CTX_PARTS = (("z", 8), ("x", 4), ("y_lo", 2))
TP_PARTS = (("y_hi", 2), ("core", 2))
CTX = tuple(name for name, _ in CTX_PARTS)
TP = tuple(name for name, _ in TP_PARTS)


def from_earlier(block, distance, count):
    route = [(i - distance, i) for i in range(count) if 0 <= i - distance < count]
    return lax.ppermute(block, CTX, route)


def to_earlier(block, distance, count):
    route = [(i, i - distance) for i in range(count) if 0 <= i - distance < count]
    return lax.ppermute(block, CTX, route)


def rotated(block, distance, count):
    route = [((i - distance) % count, i) for i in range(count)]
    return lax.ppermute(block, TP, route)


def on_device(query_rows, key_rows, value_rows, out_weight, out_grad, doc_ids, window_blocks):
    tokens_here = query_rows.shape[0]
    kv_width = key_rows.shape[1]
    kv_here = kv_width // HEAD_DIM
    groups = query_rows.shape[1] // kv_width
    score_scale = HEAD_DIM ** (-0.5)
    ctx_count = lax.axis_size(CTX)
    tp_count = lax.axis_size(TP)
    ctx_place = lax.axis_index(CTX)
    tp_place = lax.axis_index(TP)
    my_start = ctx_place * tokens_here
    span = REACH * tokens_here
    key_count = span + tokens_here

    grad_piece = lax.all_gather(out_grad, TP, axis=0, tiled=True)

    own_pair = jnp.concatenate([key_rows, value_rows], axis=1)
    earlier = [from_earlier(own_pair, distance, ctx_count) for distance in range(REACH, 0, -1)]
    pairs_all = jnp.concatenate(earlier + [own_pair], axis=0)
    keys_all = pairs_all[:, :kv_width]
    values_all = pairs_all[:, kv_width:]
    key_heads = keys_all.reshape(key_count, kv_here, HEAD_DIM)
    value_heads = values_all.reshape(key_count, kv_here, HEAD_DIM)

    doc_pad = jnp.concatenate([jnp.full((span,), -1, jnp.int32), doc_ids.astype(jnp.int32)])
    query_pos = my_start + jnp.arange(tokens_here, dtype=jnp.int32)
    key_pos = my_start - span + jnp.arange(key_count, dtype=jnp.int32)
    query_doc = lax.dynamic_slice_in_dim(doc_ids, my_start, tokens_here)
    key_doc = lax.dynamic_slice_in_dim(doc_pad, my_start, key_count)
    query_width = jnp.repeat(
        lax.dynamic_slice_in_dim(window_blocks, my_start // BLOCK, tokens_here // BLOCK), BLOCK
    )
    allowed = (
        (key_pos[None, :] >= 0)
        & (key_pos[None, :] <= query_pos[:, None])
        & (query_doc[:, None] == key_doc[None, :])
        & (query_pos[:, None] // BLOCK - key_pos[None, :] // BLOCK < query_width[:, None])
    )

    query_four = query_rows.reshape(tokens_here, kv_here, groups, HEAD_DIM)
    scores = (
        jnp.einsum("qcgd,kcd->cgqk", query_four, key_heads, preferred_element_type=jnp.float32)
        * score_scale
    )
    masked = jnp.where(allowed, scores, NEG_FILL)
    row_max = jnp.max(masked, axis=-1)
    expo = jnp.where(allowed, jnp.exp(masked - row_max[..., None]), 0.0)
    total = jnp.sum(expo, axis=-1)
    summed = jnp.einsum(
        "cgqk,kcd->qcgd", expo.astype(jnp.bfloat16), value_heads, preferred_element_type=jnp.float32
    )
    attn_four = summed / jnp.transpose(total, (2, 0, 1))[..., None]
    attn = attn_four.reshape(tokens_here, -1).astype(jnp.bfloat16)
    log_sum = row_max + jnp.log(total)

    out_part = jnp.dot(attn, out_weight, preferred_element_type=jnp.float32)
    out_chunks = out_part.reshape(tp_count, tokens_here // tp_count, out_part.shape[1])
    layer_sum = lax.dynamic_index_in_dim(out_chunks, tp_place, 0, keepdims=False)
    for distance in range(1, tp_count):
        chunk = lax.dynamic_index_in_dim(
            out_chunks, (tp_place + distance) % tp_count, 0, keepdims=False
        )
        layer_sum = layer_sum + rotated(chunk.astype(jnp.bfloat16), distance, tp_count).astype(
            jnp.float32
        )
    layer_out = layer_sum.astype(jnp.bfloat16)

    weight_part = lax.dot_general(
        attn, grad_piece, (((0,), (0,)), ((), ())), preferred_element_type=jnp.float32
    )
    weight_sum = lax.psum_scatter(
        weight_part.astype(jnp.bfloat16), CTX[0], scatter_dimension=1, tiled=True
    )
    weight_sum = lax.psum_scatter(
        weight_sum.astype(jnp.float32), CTX[1:], scatter_dimension=1, tiled=True
    )
    seq_total = ctx_count * tokens_here
    grad_weight = weight_sum * seq_total ** (-0.5)

    d_attn = lax.dot_general(
        grad_piece, out_weight, (((1,), (1,)), ((), ())), preferred_element_type=jnp.float32
    ).astype(jnp.bfloat16)
    grad_four = d_attn.reshape(tokens_here, kv_here, groups, HEAD_DIM)
    delta_rows = jnp.transpose(
        jnp.sum(
            grad_four.astype(jnp.float32)
            * attn.reshape(tokens_here, kv_here, groups, HEAD_DIM).astype(jnp.float32),
            axis=-1,
        ),
        (1, 2, 0),
    )

    probs = jnp.exp(jnp.where(allowed, scores - log_sum[..., None], NEG_FILL))
    d_probs = jnp.einsum(
        "qcgd,kcd->cgqk", grad_four, value_heads, preferred_element_type=jnp.float32
    )
    d_scores = (probs * (d_probs - delta_rows[..., None]) * score_scale).astype(jnp.bfloat16)
    query_grad = jnp.einsum(
        "cgqk,kcd->qcgd", d_scores, key_heads, preferred_element_type=jnp.float32
    )
    key_grad_all = jnp.einsum(
        "cgqk,qcgd->kcd", d_scores, query_four, preferred_element_type=jnp.float32
    ).reshape(key_count, kv_width)
    value_grad_all = jnp.einsum(
        "cgqk,qcgd->kcd", probs.astype(jnp.bfloat16), grad_four, preferred_element_type=jnp.float32
    ).reshape(key_count, kv_width)

    pair_grad_all = jnp.concatenate([key_grad_all, value_grad_all], axis=1)
    pair_grad = pair_grad_all[span:]
    for distance in range(1, REACH + 1):
        lo = span - distance * tokens_here
        sent = to_earlier(
            pair_grad_all[lo : lo + tokens_here].astype(jnp.bfloat16), distance, ctx_count
        )
        pair_grad = pair_grad + sent.astype(jnp.float32)
    key_grad = pair_grad[:, :kv_width]
    value_grad = pair_grad[:, kv_width:]

    grad_queries = query_grad.reshape(tokens_here, -1).astype(jnp.bfloat16)
    grad_keys = key_grad.astype(jnp.bfloat16)
    grad_values = value_grad.astype(jnp.bfloat16)
    return (layer_out, grad_queries, grad_keys, grad_values, grad_weight)


def solution(mesh):
    shape = tuple(size for _, size in CTX_PARTS + TP_PARTS)
    fine = Mesh(np.asarray(mesh.devices).reshape(shape), CTX + TP)
    placed = (
        P(CTX, TP),
        P(CTX, TP),
        P(CTX, TP),
        P(TP, None),
        P(CTX + TP, None),
        P(),
        P(),
    )
    return jax.shard_map(
        on_device,
        mesh=fine,
        in_specs=placed,
        out_specs=(
            P(CTX + TP, None),
            P(CTX, TP),
            P(CTX, TP),
            P(CTX, TP),
            P(TP, CTX),
        ),
        check_vma=False,
    )
```

```python
import jax
import jax.numpy as jnp
import numpy as np
from jax import lax
from jax.sharding import Mesh
from jax.sharding import PartitionSpec as P

HEAD_DIM = 128
BLOCK = 128
REACH = 3
NEG_FILL = -1e30

CTX_PARTS = (("z", 8), ("x", 4), ("y_lo", 2))
TP_PARTS = (("y_hi", 2), ("core", 2))
CTX = tuple(name for name, _ in CTX_PARTS)
TP = tuple(name for name, _ in TP_PARTS)


def from_earlier(block, distance, count):
    route = [(i - distance, i) for i in range(count) if 0 <= i - distance < count]
    return lax.ppermute(block, CTX, route)


def to_earlier(block, distance, count):
    route = [(i, i - distance) for i in range(count) if 0 <= i - distance < count]
    return lax.ppermute(block, CTX, route)


def swapped(block, axis):
    return lax.ppermute(block, axis, [(0, 1), (1, 0)])


def in_order(own, other, place):
    first = jnp.where(place == 0, own, other)
    second = jnp.where(place == 0, other, own)
    return jnp.stack([first, second])


def gathered_over_tp(piece):
    high = lax.axis_index(TP[0])
    low = lax.axis_index(TP[1])
    by_high = in_order(piece, swapped(piece, TP[0]), high)
    both = in_order(by_high, swapped(by_high, TP[1]), low)
    return jnp.transpose(both, (1, 0, 2, 3)).reshape(-1, piece.shape[1])


def summed_over_tp(part):
    high = lax.axis_index(TP[0])
    low = lax.axis_index(TP[1])
    quarters = part.reshape(2, 2, part.shape[0] // 4, part.shape[1])
    kept = lax.dynamic_index_in_dim(quarters, low, 1, keepdims=False)
    given = lax.dynamic_index_in_dim(quarters, 1 - low, 1, keepdims=False)
    halves = kept + swapped(given.astype(jnp.bfloat16), TP[1]).astype(jnp.float32)
    kept = lax.dynamic_index_in_dim(halves, high, 0, keepdims=False)
    given = lax.dynamic_index_in_dim(halves, 1 - high, 0, keepdims=False)
    return kept + swapped(given.astype(jnp.bfloat16), TP[0]).astype(jnp.float32)


def on_device(query_rows, key_rows, value_rows, out_weight, out_grad, doc_ids, window_blocks):
    tokens_here = query_rows.shape[0]
    kv_width = key_rows.shape[1]
    kv_here = kv_width // HEAD_DIM
    groups = query_rows.shape[1] // kv_width
    score_scale = HEAD_DIM ** (-0.5)
    ctx_count = lax.axis_size(CTX)
    ctx_place = lax.axis_index(CTX)
    my_start = ctx_place * tokens_here
    span = REACH * tokens_here
    key_count = span + tokens_here

    grad_piece = gathered_over_tp(out_grad)

    own_pair = jnp.concatenate([key_rows, value_rows], axis=1)
    earlier = [from_earlier(own_pair, distance, ctx_count) for distance in range(REACH, 0, -1)]
    pairs_all = jnp.concatenate(earlier + [own_pair], axis=0)
    keys_all = pairs_all[:, :kv_width]
    values_all = pairs_all[:, kv_width:]
    key_heads = keys_all.reshape(key_count, kv_here, HEAD_DIM)
    value_heads = values_all.reshape(key_count, kv_here, HEAD_DIM)

    doc_pad = jnp.concatenate([jnp.full((span,), -1, jnp.int32), doc_ids.astype(jnp.int32)])
    query_pos = my_start + jnp.arange(tokens_here, dtype=jnp.int32)
    key_pos = my_start - span + jnp.arange(key_count, dtype=jnp.int32)
    query_doc = lax.dynamic_slice_in_dim(doc_ids, my_start, tokens_here)
    key_doc = lax.dynamic_slice_in_dim(doc_pad, my_start, key_count)
    query_width = jnp.repeat(
        lax.dynamic_slice_in_dim(window_blocks, my_start // BLOCK, tokens_here // BLOCK), BLOCK
    )
    allowed = (
        (key_pos[None, :] >= 0)
        & (key_pos[None, :] <= query_pos[:, None])
        & (query_doc[:, None] == key_doc[None, :])
        & (query_pos[:, None] // BLOCK - key_pos[None, :] // BLOCK < query_width[:, None])
    )

    query_four = query_rows.reshape(tokens_here, kv_here, groups, HEAD_DIM)
    scores = (
        jnp.einsum("qcgd,kcd->cgqk", query_four, key_heads, preferred_element_type=jnp.float32)
        * score_scale
    )
    masked = jnp.where(allowed, scores, NEG_FILL)
    row_max = jnp.max(masked, axis=-1)
    expo = jnp.where(allowed, jnp.exp(masked - row_max[..., None]), 0.0)
    total = jnp.sum(expo, axis=-1)
    summed = jnp.einsum(
        "cgqk,kcd->qcgd", expo.astype(jnp.bfloat16), value_heads, preferred_element_type=jnp.float32
    )
    attn_four = summed / jnp.transpose(total, (2, 0, 1))[..., None]
    attn = attn_four.reshape(tokens_here, -1).astype(jnp.bfloat16)
    log_sum = row_max + jnp.log(total)

    out_part = jnp.dot(attn, out_weight, preferred_element_type=jnp.float32)
    layer_out = summed_over_tp(out_part).astype(jnp.bfloat16)

    weight_part = lax.dot_general(
        attn, grad_piece, (((0,), (0,)), ((), ())), preferred_element_type=jnp.float32
    )
    weight_sum = lax.psum_scatter(
        weight_part.astype(jnp.bfloat16), CTX[0], scatter_dimension=1, tiled=True
    )
    rest_count = ctx_count // lax.axis_size(CTX[0])
    weight_cols = weight_sum.reshape(weight_sum.shape[0], rest_count, -1).transpose(1, 0, 2)
    weight_cols = lax.all_to_all(weight_cols, CTX[1:], 0, 0, tiled=True)
    weight_sum = jnp.sum(weight_cols.astype(jnp.float32), axis=0)
    seq_total = ctx_count * tokens_here
    grad_weight = weight_sum * seq_total ** (-0.5)

    d_attn = lax.dot_general(
        grad_piece, out_weight, (((1,), (1,)), ((), ())), preferred_element_type=jnp.float32
    ).astype(jnp.bfloat16)
    grad_four = d_attn.reshape(tokens_here, kv_here, groups, HEAD_DIM)
    delta_rows = jnp.transpose(
        jnp.sum(
            grad_four.astype(jnp.float32)
            * attn.reshape(tokens_here, kv_here, groups, HEAD_DIM).astype(jnp.float32),
            axis=-1,
        ),
        (1, 2, 0),
    )

    probs = jnp.exp(jnp.where(allowed, scores - log_sum[..., None], NEG_FILL))
    d_probs = jnp.einsum(
        "qcgd,kcd->cgqk", grad_four, value_heads, preferred_element_type=jnp.float32
    )
    d_scores = (probs * (d_probs - delta_rows[..., None]) * score_scale).astype(jnp.bfloat16)
    query_grad = jnp.einsum(
        "cgqk,kcd->qcgd", d_scores, key_heads, preferred_element_type=jnp.float32
    )
    key_grad_all = jnp.einsum(
        "cgqk,qcgd->kcd", d_scores, query_four, preferred_element_type=jnp.float32
    ).reshape(key_count, kv_width)
    value_grad_all = jnp.einsum(
        "cgqk,qcgd->kcd", probs.astype(jnp.bfloat16), grad_four, preferred_element_type=jnp.float32
    ).reshape(key_count, kv_width)

    pair_grad_all = jnp.concatenate([key_grad_all, value_grad_all], axis=1)
    pair_grad = pair_grad_all[span:]
    for distance in range(1, REACH + 1):
        lo = span - distance * tokens_here
        sent = to_earlier(
            pair_grad_all[lo : lo + tokens_here].astype(jnp.bfloat16), distance, ctx_count
        )
        pair_grad = pair_grad + sent.astype(jnp.float32)
    key_grad = pair_grad[:, :kv_width]
    value_grad = pair_grad[:, kv_width:]

    grad_queries = query_grad.reshape(tokens_here, -1).astype(jnp.bfloat16)
    grad_keys = key_grad.astype(jnp.bfloat16)
    grad_values = value_grad.astype(jnp.bfloat16)
    return (layer_out, grad_queries, grad_keys, grad_values, grad_weight)


def solution(mesh):
    shape = tuple(size for _, size in CTX_PARTS + TP_PARTS)
    fine = Mesh(np.asarray(mesh.devices).reshape(shape), CTX + TP)
    placed = (
        P(CTX, TP),
        P(CTX, TP),
        P(CTX, TP),
        P(TP, None),
        P(CTX + TP, None),
        P(),
        P(),
    )
    return jax.shard_map(
        on_device,
        mesh=fine,
        in_specs=placed,
        out_specs=(
            P(CTX + TP, None),
            P(CTX, TP),
            P(CTX, TP),
            P(CTX, TP),
            P(TP, CTX),
        ),
        check_vma=False,
    )
```

```python
import jax
import jax.numpy as jnp
import numpy as np
from jax import lax
from jax.sharding import Mesh
from jax.sharding import PartitionSpec as P

HEAD_DIM = 128
BLOCK = 128
REACH = 3
NEG_FILL = -1e30

CTX_PARTS = (("z", 8), ("x", 4), ("y_lo", 2))
TP_PARTS = (("y_hi", 2), ("core", 2))
CTX = tuple(name for name, _ in CTX_PARTS)
TP = tuple(name for name, _ in TP_PARTS)


def from_earlier(block, distance, count):
    route = [(i - distance, i) for i in range(count) if 0 <= i - distance < count]
    return lax.ppermute(block, CTX, route)


def to_earlier(block, distance, count):
    route = [(i, i - distance) for i in range(count) if 0 <= i - distance < count]
    return lax.ppermute(block, CTX, route)


def swapped(block, axis):
    return lax.ppermute(block, axis, [(0, 1), (1, 0)])


def in_order(own, other, place):
    first = jnp.where(place == 0, own, other)
    second = jnp.where(place == 0, other, own)
    return jnp.stack([first, second])


def gathered_over_tp(piece):
    high = lax.axis_index(TP[0])
    low = lax.axis_index(TP[1])
    by_high = in_order(piece, swapped(piece, TP[0]), high)
    both = in_order(by_high, swapped(by_high, TP[1]), low)
    return jnp.transpose(both, (1, 0, 2, 3)).reshape(-1, piece.shape[1])


def summed_over_tp(part):
    high = lax.axis_index(TP[0])
    low = lax.axis_index(TP[1])
    quarters = part.reshape(2, 2, part.shape[0] // 4, part.shape[1])
    kept = lax.dynamic_index_in_dim(quarters, low, 1, keepdims=False)
    given = lax.dynamic_index_in_dim(quarters, 1 - low, 1, keepdims=False)
    halves = kept + swapped(given.astype(jnp.bfloat16), TP[1]).astype(jnp.float32)
    kept = lax.dynamic_index_in_dim(halves, high, 0, keepdims=False)
    given = lax.dynamic_index_in_dim(halves, 1 - high, 0, keepdims=False)
    return kept + swapped(given.astype(jnp.bfloat16), TP[0]).astype(jnp.float32)


def on_device(query_rows, key_rows, value_rows, out_weight, out_grad, doc_ids, window_blocks):
    tokens_here = query_rows.shape[0]
    kv_width = key_rows.shape[1]
    kv_here = kv_width // HEAD_DIM
    groups = query_rows.shape[1] // kv_width
    score_scale = HEAD_DIM ** (-0.5)
    ctx_count = lax.axis_size(CTX)
    ctx_place = lax.axis_index(CTX)
    my_start = ctx_place * tokens_here
    span = REACH * tokens_here
    key_count = span + tokens_here

    grad_piece = gathered_over_tp(out_grad)

    own_pair = jnp.concatenate([key_rows, value_rows], axis=1)
    earlier = [from_earlier(own_pair, distance, ctx_count) for distance in range(REACH, 0, -1)]
    pairs_all = jnp.concatenate(earlier + [own_pair], axis=0)
    keys_all = pairs_all[:, :kv_width]
    values_all = pairs_all[:, kv_width:]
    key_heads = keys_all.reshape(key_count, kv_here, HEAD_DIM)
    value_heads = values_all.reshape(key_count, kv_here, HEAD_DIM)

    doc_pad = jnp.concatenate([jnp.full((span,), -1, jnp.int32), doc_ids.astype(jnp.int32)])
    query_pos = my_start + jnp.arange(tokens_here, dtype=jnp.int32)
    key_pos = my_start - span + jnp.arange(key_count, dtype=jnp.int32)
    query_doc = lax.dynamic_slice_in_dim(doc_ids, my_start, tokens_here)
    key_doc = lax.dynamic_slice_in_dim(doc_pad, my_start, key_count)
    query_width = jnp.repeat(
        lax.dynamic_slice_in_dim(window_blocks, my_start // BLOCK, tokens_here // BLOCK), BLOCK
    )
    allowed = (
        (key_pos[None, :] >= 0)
        & (key_pos[None, :] <= query_pos[:, None])
        & (query_doc[:, None] == key_doc[None, :])
        & (query_pos[:, None] // BLOCK - key_pos[None, :] // BLOCK < query_width[:, None])
    )

    query_four = query_rows.reshape(tokens_here, kv_here, groups, HEAD_DIM)
    scores = (
        jnp.einsum("qcgd,kcd->cgqk", query_four, key_heads, preferred_element_type=jnp.float32)
        * score_scale
    )
    masked = jnp.where(allowed, scores, NEG_FILL)
    row_max = jnp.max(masked, axis=-1)
    expo = jnp.where(allowed, jnp.exp(masked - row_max[..., None]), 0.0)
    total = jnp.sum(expo, axis=-1)
    summed = jnp.einsum(
        "cgqk,kcd->qcgd", expo.astype(jnp.bfloat16), value_heads, preferred_element_type=jnp.float32
    )
    attn_four = summed / jnp.transpose(total, (2, 0, 1))[..., None]
    attn = attn_four.reshape(tokens_here, -1).astype(jnp.bfloat16)
    log_sum = row_max + jnp.log(total)

    weight_part = lax.dot_general(
        attn, grad_piece, (((0,), (0,)), ((), ())), preferred_element_type=jnp.float32
    ).astype(jnp.bfloat16)
    weight_part, attn, grad_piece = lax.optimization_barrier((weight_part, attn, grad_piece))
    weight_sum = lax.psum_scatter(weight_part, CTX[0], scatter_dimension=1, tiled=True)

    out_part = jnp.dot(attn, out_weight, preferred_element_type=jnp.float32)
    layer_out = summed_over_tp(out_part).astype(jnp.bfloat16)
    rest_count = ctx_count // lax.axis_size(CTX[0])
    weight_cols = weight_sum.reshape(weight_sum.shape[0], rest_count, -1).transpose(1, 0, 2)
    weight_cols = lax.all_to_all(weight_cols, CTX[1:], 0, 0, tiled=True)
    weight_sum = jnp.sum(weight_cols.astype(jnp.float32), axis=0)
    seq_total = ctx_count * tokens_here
    grad_weight = weight_sum * seq_total ** (-0.5)

    d_attn = lax.dot_general(
        grad_piece, out_weight, (((1,), (1,)), ((), ())), preferred_element_type=jnp.float32
    ).astype(jnp.bfloat16)
    grad_four = d_attn.reshape(tokens_here, kv_here, groups, HEAD_DIM)
    delta_rows = jnp.transpose(
        jnp.sum(
            grad_four.astype(jnp.float32)
            * attn.reshape(tokens_here, kv_here, groups, HEAD_DIM).astype(jnp.float32),
            axis=-1,
        ),
        (1, 2, 0),
    )

    probs = jnp.exp(jnp.where(allowed, scores - log_sum[..., None], NEG_FILL))
    d_probs = jnp.einsum(
        "qcgd,kcd->cgqk", grad_four, value_heads, preferred_element_type=jnp.float32
    )
    d_scores = (probs * (d_probs - delta_rows[..., None]) * score_scale).astype(jnp.bfloat16)
    query_grad = jnp.einsum(
        "cgqk,kcd->qcgd", d_scores, key_heads, preferred_element_type=jnp.float32
    )
    key_grad_all = jnp.einsum(
        "cgqk,qcgd->kcd", d_scores, query_four, preferred_element_type=jnp.float32
    ).reshape(key_count, kv_width)
    value_grad_all = jnp.einsum(
        "cgqk,qcgd->kcd", probs.astype(jnp.bfloat16), grad_four, preferred_element_type=jnp.float32
    ).reshape(key_count, kv_width)

    pair_grad_all = jnp.concatenate([key_grad_all, value_grad_all], axis=1)
    pair_grad = pair_grad_all[span:]
    for distance in range(1, REACH + 1):
        lo = span - distance * tokens_here
        sent = to_earlier(
            pair_grad_all[lo : lo + tokens_here].astype(jnp.bfloat16), distance, ctx_count
        )
        pair_grad = pair_grad + sent.astype(jnp.float32)
    key_grad = pair_grad[:, :kv_width]
    value_grad = pair_grad[:, kv_width:]

    grad_queries = query_grad.reshape(tokens_here, -1).astype(jnp.bfloat16)
    grad_keys = key_grad.astype(jnp.bfloat16)
    grad_values = value_grad.astype(jnp.bfloat16)
    return (layer_out, grad_queries, grad_keys, grad_values, grad_weight)


def solution(mesh):
    shape = tuple(size for _, size in CTX_PARTS + TP_PARTS)
    fine = Mesh(np.asarray(mesh.devices).reshape(shape), CTX + TP)
    placed = (
        P(CTX, TP),
        P(CTX, TP),
        P(CTX, TP),
        P(TP, None),
        P(CTX + TP, None),
        P(),
        P(),
    )
    return jax.shard_map(
        on_device,
        mesh=fine,
        in_specs=placed,
        out_specs=(
            P(CTX + TP, None),
            P(CTX, TP),
            P(CTX, TP),
            P(CTX, TP),
            P(TP, CTX),
        ),
        check_vma=False,
    )
```

```python
import jax
import jax.numpy as jnp
import numpy as np
from jax import lax
from jax.sharding import Mesh
from jax.sharding import PartitionSpec as P

HEAD_DIM = 128
BLOCK = 128
REACH = 3
NEG_FILL = -1e30

CTX_PARTS = (("z", 8), ("x", 4), ("y_lo", 2))
TP_PARTS = (("y_hi", 2), ("core", 2))
CTX = tuple(name for name, _ in CTX_PARTS)
TP = tuple(name for name, _ in TP_PARTS)


def from_earlier(block, distance, count):
    route = [(i - distance, i) for i in range(count) if 0 <= i - distance < count]
    return lax.ppermute(block, CTX, route)


def to_earlier(block, distance, count):
    route = [(i, i - distance) for i in range(count) if 0 <= i - distance < count]
    return lax.ppermute(block, CTX, route)


def swapped(block, axis):
    return lax.ppermute(block, axis, [(0, 1), (1, 0)])


def in_order(own, other, place):
    first = jnp.where(place == 0, own, other)
    second = jnp.where(place == 0, other, own)
    return jnp.stack([first, second])


def gathered_over_tp(piece, after):
    high = lax.axis_index(TP[0])
    low = lax.axis_index(TP[1])
    other, after = lax.optimization_barrier((swapped(piece, TP[0]), after))
    by_high = in_order(piece, other, high)
    both = in_order(by_high, swapped(by_high, TP[1]), low)
    return jnp.transpose(both, (1, 0, 2, 3)).reshape(-1, piece.shape[1]), after


def summed_over_tp(part):
    high = lax.axis_index(TP[0])
    low = lax.axis_index(TP[1])
    quarters = part.reshape(2, 2, part.shape[0] // 4, part.shape[1])
    kept = lax.dynamic_index_in_dim(quarters, low, 1, keepdims=False)
    given = lax.dynamic_index_in_dim(quarters, 1 - low, 1, keepdims=False)
    halves = kept + swapped(given.astype(jnp.bfloat16), TP[1]).astype(jnp.float32)
    kept = lax.dynamic_index_in_dim(halves, high, 0, keepdims=False)
    given = lax.dynamic_index_in_dim(halves, 1 - high, 0, keepdims=False)
    return kept + swapped(given.astype(jnp.bfloat16), TP[0]).astype(jnp.float32)


def on_device(query_rows, key_rows, value_rows, out_weight, out_grad, doc_ids, window_blocks):
    tokens_here = query_rows.shape[0]
    kv_width = key_rows.shape[1]
    kv_here = kv_width // HEAD_DIM
    groups = query_rows.shape[1] // kv_width
    score_scale = HEAD_DIM ** (-0.5)
    ctx_count = lax.axis_size(CTX)
    ctx_place = lax.axis_index(CTX)
    my_start = ctx_place * tokens_here
    span = REACH * tokens_here
    key_count = span + tokens_here

    own_pair = jnp.concatenate([key_rows, value_rows], axis=1)
    earlier = [from_earlier(own_pair, distance, ctx_count) for distance in range(REACH, 0, -1)]
    pairs_all = jnp.concatenate(earlier + [own_pair], axis=0)
    keys_all = pairs_all[:, :kv_width]
    values_all = pairs_all[:, kv_width:]
    key_heads = keys_all.reshape(key_count, kv_here, HEAD_DIM)
    value_heads = values_all.reshape(key_count, kv_here, HEAD_DIM)

    doc_pad = jnp.concatenate([jnp.full((span,), -1, jnp.int32), doc_ids.astype(jnp.int32)])
    query_pos = my_start + jnp.arange(tokens_here, dtype=jnp.int32)
    key_pos = my_start - span + jnp.arange(key_count, dtype=jnp.int32)
    query_doc = lax.dynamic_slice_in_dim(doc_ids, my_start, tokens_here)
    key_doc = lax.dynamic_slice_in_dim(doc_pad, my_start, key_count)
    query_width = jnp.repeat(
        lax.dynamic_slice_in_dim(window_blocks, my_start // BLOCK, tokens_here // BLOCK), BLOCK
    )
    allowed = (
        (key_pos[None, :] >= 0)
        & (key_pos[None, :] <= query_pos[:, None])
        & (query_doc[:, None] == key_doc[None, :])
        & (query_pos[:, None] // BLOCK - key_pos[None, :] // BLOCK < query_width[:, None])
    )

    query_four = query_rows.reshape(tokens_here, kv_here, groups, HEAD_DIM)
    scores = (
        jnp.einsum("qcgd,kcd->cgqk", query_four, key_heads, preferred_element_type=jnp.float32)
        * score_scale
    )
    masked = jnp.where(allowed, scores, NEG_FILL)
    row_max = jnp.max(masked, axis=-1)
    expo = jnp.where(allowed, jnp.exp(masked - row_max[..., None]), 0.0)
    total = jnp.sum(expo, axis=-1)
    summed = jnp.einsum(
        "cgqk,kcd->qcgd", expo.astype(jnp.bfloat16), value_heads, preferred_element_type=jnp.float32
    )
    attn_four = summed / jnp.transpose(total, (2, 0, 1))[..., None]
    attn = attn_four.reshape(tokens_here, -1).astype(jnp.bfloat16)
    log_sum = row_max + jnp.log(total)
    grad_piece, attn = gathered_over_tp(out_grad, attn)

    weight_part = lax.dot_general(
        attn, grad_piece, (((0,), (0,)), ((), ())), preferred_element_type=jnp.float32
    ).astype(jnp.bfloat16)
    weight_part, attn, grad_piece = lax.optimization_barrier((weight_part, attn, grad_piece))
    weight_sum = lax.psum_scatter(weight_part, CTX[0], scatter_dimension=1, tiled=True)

    out_part = jnp.dot(attn, out_weight, preferred_element_type=jnp.float32)
    layer_out = summed_over_tp(out_part).astype(jnp.bfloat16)
    rest_count = ctx_count // lax.axis_size(CTX[0])
    weight_cols = weight_sum.reshape(weight_sum.shape[0], rest_count, -1).transpose(1, 0, 2)
    weight_cols = lax.all_to_all(weight_cols, CTX[1:], 0, 0, tiled=True)
    weight_sum = jnp.sum(weight_cols.astype(jnp.float32), axis=0)
    seq_total = ctx_count * tokens_here
    grad_weight = weight_sum * seq_total ** (-0.5)

    d_attn = lax.dot_general(
        grad_piece, out_weight, (((1,), (1,)), ((), ())), preferred_element_type=jnp.float32
    ).astype(jnp.bfloat16)
    grad_four = d_attn.reshape(tokens_here, kv_here, groups, HEAD_DIM)
    delta_rows = jnp.transpose(
        jnp.sum(
            grad_four.astype(jnp.float32)
            * attn.reshape(tokens_here, kv_here, groups, HEAD_DIM).astype(jnp.float32),
            axis=-1,
        ),
        (1, 2, 0),
    )

    probs = jnp.exp(jnp.where(allowed, scores - log_sum[..., None], NEG_FILL))
    d_probs = jnp.einsum(
        "qcgd,kcd->cgqk", grad_four, value_heads, preferred_element_type=jnp.float32
    )
    d_scores = (probs * (d_probs - delta_rows[..., None]) * score_scale).astype(jnp.bfloat16)
    probs_half = probs.astype(jnp.bfloat16)

    def key_side(score_part, prob_part):
        key_part = jnp.einsum(
            "cgqk,qcgd->kcd", score_part, query_four, preferred_element_type=jnp.float32
        )
        value_part = jnp.einsum(
            "cgqk,qcgd->kcd", prob_part, grad_four, preferred_element_type=jnp.float32
        )
        rows = score_part.shape[-1]
        return jnp.concatenate(
            [key_part.reshape(rows, kv_width), value_part.reshape(rows, kv_width)], axis=1
        )

    early_grad = key_side(d_scores[..., :span], probs_half[..., :span]).astype(jnp.bfloat16)
    early_grad, d_scores, probs_half = lax.optimization_barrier((early_grad, d_scores, probs_half))
    returned = []
    for distance in range(1, REACH + 1):
        lo = span - distance * tokens_here
        returned.append(to_earlier(early_grad[lo : lo + tokens_here], distance, ctx_count))
    query_grad = jnp.einsum(
        "cgqk,kcd->qcgd", d_scores, key_heads, preferred_element_type=jnp.float32
    )
    pair_grad = key_side(d_scores[..., span:], probs_half[..., span:])
    for sent in returned:
        pair_grad = pair_grad + sent.astype(jnp.float32)
    key_grad = pair_grad[:, :kv_width]
    value_grad = pair_grad[:, kv_width:]

    grad_queries = query_grad.reshape(tokens_here, -1).astype(jnp.bfloat16)
    grad_keys = key_grad.astype(jnp.bfloat16)
    grad_values = value_grad.astype(jnp.bfloat16)
    return (layer_out, grad_queries, grad_keys, grad_values, grad_weight)


def solution(mesh):
    shape = tuple(size for _, size in CTX_PARTS + TP_PARTS)
    fine = Mesh(np.asarray(mesh.devices).reshape(shape), CTX + TP)
    placed = (
        P(CTX, TP),
        P(CTX, TP),
        P(CTX, TP),
        P(TP, None),
        P(CTX + TP, None),
        P(),
        P(),
    )
    return jax.shard_map(
        on_device,
        mesh=fine,
        in_specs=placed,
        out_specs=(
            P(CTX + TP, None),
            P(CTX, TP),
            P(CTX, TP),
            P(CTX, TP),
            P(TP, CTX),
        ),
        check_vma=False,
    )
```

```python
import jax
import jax.numpy as jnp
import numpy as np
from jax import lax
from jax.sharding import Mesh
from jax.sharding import PartitionSpec as P

HEAD_DIM = 128
BLOCK = 128
REACH = 3
NEG_FILL = -1e30

CTX_PARTS = (("z", 8), ("x", 4), ("y_lo", 2))
TP_PARTS = (("y_hi", 2), ("core", 2))
CTX = tuple(name for name, _ in CTX_PARTS)
TP = tuple(name for name, _ in TP_PARTS)


def from_earlier(block, distance, count):
    route = [(i - distance, i) for i in range(count) if 0 <= i - distance < count]
    return lax.ppermute(block, CTX, route)


def to_earlier(block, distance, count):
    route = [(i, i - distance) for i in range(count) if 0 <= i - distance < count]
    return lax.ppermute(block, CTX, route)


def swapped(block, axis):
    return lax.ppermute(block, axis, [(0, 1), (1, 0)])


def in_order(own, other, place):
    first = jnp.where(place == 0, own, other)
    second = jnp.where(place == 0, other, own)
    return jnp.stack([first, second])


def gathered_over_tp(piece, after):
    high = lax.axis_index(TP[0])
    low = lax.axis_index(TP[1])
    other, after = lax.optimization_barrier((swapped(piece, TP[0]), after))
    by_high = in_order(piece, other, high)
    both = in_order(by_high, swapped(by_high, TP[1]), low)
    return jnp.transpose(both, (1, 0, 2, 3)).reshape(-1, piece.shape[1]), after


def summed_over_tp(part):
    high = lax.axis_index(TP[0])
    low = lax.axis_index(TP[1])
    quarters = part.reshape(2, 2, part.shape[0] // 4, part.shape[1])
    kept = lax.dynamic_index_in_dim(quarters, low, 1, keepdims=False)
    given = lax.dynamic_index_in_dim(quarters, 1 - low, 1, keepdims=False)
    halves = kept + swapped(given.astype(jnp.bfloat16), TP[1]).astype(jnp.float32)
    kept = lax.dynamic_index_in_dim(halves, high, 0, keepdims=False)
    given = lax.dynamic_index_in_dim(halves, 1 - high, 0, keepdims=False)
    return kept, swapped(given.astype(jnp.bfloat16), TP[0])


def on_device(query_rows, key_rows, value_rows, out_weight, out_grad, doc_ids, window_blocks):
    tokens_here = query_rows.shape[0]
    kv_width = key_rows.shape[1]
    kv_here = kv_width // HEAD_DIM
    groups = query_rows.shape[1] // kv_width
    score_scale = HEAD_DIM ** (-0.5)
    ctx_count = lax.axis_size(CTX)
    ctx_place = lax.axis_index(CTX)
    my_start = ctx_place * tokens_here
    span = REACH * tokens_here
    key_count = span + tokens_here

    own_pair = jnp.concatenate([key_rows, value_rows], axis=1)
    earlier = [from_earlier(own_pair, distance, ctx_count) for distance in range(REACH, 0, -1)]
    pairs_all = jnp.concatenate(earlier + [own_pair], axis=0)
    keys_all = pairs_all[:, :kv_width]
    values_all = pairs_all[:, kv_width:]
    key_heads = keys_all.reshape(key_count, kv_here, HEAD_DIM)
    value_heads = values_all.reshape(key_count, kv_here, HEAD_DIM)

    doc_pad = jnp.concatenate([jnp.full((span,), -1, jnp.int32), doc_ids.astype(jnp.int32)])
    query_pos = my_start + jnp.arange(tokens_here, dtype=jnp.int32)
    key_pos = my_start - span + jnp.arange(key_count, dtype=jnp.int32)
    query_doc = lax.dynamic_slice_in_dim(doc_ids, my_start, tokens_here)
    key_doc = lax.dynamic_slice_in_dim(doc_pad, my_start, key_count)
    query_width = jnp.repeat(
        lax.dynamic_slice_in_dim(window_blocks, my_start // BLOCK, tokens_here // BLOCK), BLOCK
    )
    allowed = (
        (key_pos[None, :] >= 0)
        & (key_pos[None, :] <= query_pos[:, None])
        & (query_doc[:, None] == key_doc[None, :])
        & (query_pos[:, None] // BLOCK - key_pos[None, :] // BLOCK < query_width[:, None])
    )

    query_four = query_rows.reshape(tokens_here, kv_here, groups, HEAD_DIM)
    scores = (
        jnp.einsum("qcgd,kcd->cgqk", query_four, key_heads, preferred_element_type=jnp.float32)
        * score_scale
    )
    masked = jnp.where(allowed, scores, NEG_FILL)
    row_max = jnp.max(masked, axis=-1)
    expo = jnp.where(allowed, jnp.exp(masked - row_max[..., None]), 0.0)
    total = jnp.sum(expo, axis=-1)
    summed = jnp.einsum(
        "cgqk,kcd->qcgd", expo.astype(jnp.bfloat16), value_heads, preferred_element_type=jnp.float32
    )
    attn_four = summed / jnp.transpose(total, (2, 0, 1))[..., None]
    attn = attn_four.reshape(tokens_here, -1).astype(jnp.bfloat16)
    log_sum = row_max + jnp.log(total)
    grad_piece, attn = gathered_over_tp(out_grad, attn)

    weight_part = lax.dot_general(
        attn, grad_piece, (((0,), (0,)), ((), ())), preferred_element_type=jnp.float32
    ).astype(jnp.bfloat16)
    weight_part, attn, grad_piece = lax.optimization_barrier((weight_part, attn, grad_piece))
    weight_sum = lax.psum_scatter(weight_part, CTX[0], scatter_dimension=1, tiled=True)

    out_part = jnp.dot(attn, out_weight, preferred_element_type=jnp.float32)
    layer_kept, layer_received = summed_over_tp(out_part)
    rest_count = ctx_count // lax.axis_size(CTX[0])
    weight_cols = weight_sum.reshape(weight_sum.shape[0], rest_count, -1).transpose(1, 0, 2)
    weight_cols = lax.all_to_all(weight_cols, CTX[1:], 0, 0, tiled=True)
    weight_sum = jnp.sum(weight_cols.astype(jnp.float32), axis=0)
    seq_total = ctx_count * tokens_here
    grad_weight = weight_sum * seq_total ** (-0.5)

    d_attn = lax.dot_general(
        grad_piece, out_weight, (((1,), (1,)), ((), ())), preferred_element_type=jnp.float32
    ).astype(jnp.bfloat16)
    grad_four = d_attn.reshape(tokens_here, kv_here, groups, HEAD_DIM)
    delta_rows = jnp.transpose(
        jnp.sum(
            grad_four.astype(jnp.float32)
            * attn.reshape(tokens_here, kv_here, groups, HEAD_DIM).astype(jnp.float32),
            axis=-1,
        ),
        (1, 2, 0),
    )

    probs = jnp.exp(jnp.where(allowed, scores - log_sum[..., None], NEG_FILL))
    d_probs = jnp.einsum(
        "qcgd,kcd->cgqk", grad_four, value_heads, preferred_element_type=jnp.float32
    )
    d_scores = (probs * (d_probs - delta_rows[..., None]) * score_scale).astype(jnp.bfloat16)
    layer_received, d_scores = lax.optimization_barrier((layer_received, d_scores))
    layer_out = (layer_kept + layer_received.astype(jnp.float32)).astype(jnp.bfloat16)
    probs_half = probs.astype(jnp.bfloat16)

    def key_side(score_part, prob_part):
        key_part = jnp.einsum(
            "cgqk,qcgd->kcd", score_part, query_four, preferred_element_type=jnp.float32
        )
        value_part = jnp.einsum(
            "cgqk,qcgd->kcd", prob_part, grad_four, preferred_element_type=jnp.float32
        )
        rows = score_part.shape[-1]
        return jnp.concatenate(
            [key_part.reshape(rows, kv_width), value_part.reshape(rows, kv_width)], axis=1
        )

    early_grad = key_side(d_scores[..., :span], probs_half[..., :span]).astype(jnp.bfloat16)
    early_grad, d_scores, probs_half = lax.optimization_barrier((early_grad, d_scores, probs_half))
    returned = []
    for distance in range(1, REACH + 1):
        lo = span - distance * tokens_here
        returned.append(to_earlier(early_grad[lo : lo + tokens_here], distance, ctx_count))
    query_grad = jnp.einsum(
        "cgqk,kcd->qcgd", d_scores, key_heads, preferred_element_type=jnp.float32
    )
    pair_grad = key_side(d_scores[..., span:], probs_half[..., span:])
    for sent in returned:
        pair_grad = pair_grad + sent.astype(jnp.float32)
    key_grad = pair_grad[:, :kv_width]
    value_grad = pair_grad[:, kv_width:]

    grad_queries = query_grad.reshape(tokens_here, -1).astype(jnp.bfloat16)
    grad_keys = key_grad.astype(jnp.bfloat16)
    grad_values = value_grad.astype(jnp.bfloat16)
    return (layer_out, grad_queries, grad_keys, grad_values, grad_weight)


def solution(mesh):
    shape = tuple(size for _, size in CTX_PARTS + TP_PARTS)
    fine = Mesh(np.asarray(mesh.devices).reshape(shape), CTX + TP)
    placed = (
        P(CTX, TP),
        P(CTX, TP),
        P(CTX, TP),
        P(TP, None),
        P(CTX + TP, None),
        P(),
        P(),
    )
    return jax.shard_map(
        on_device,
        mesh=fine,
        in_specs=placed,
        out_specs=(
            P(CTX + TP, None),
            P(CTX, TP),
            P(CTX, TP),
            P(CTX, TP),
            P(TP, CTX),
        ),
        check_vma=False,
    )
```

```python
import jax
import jax.numpy as jnp
import numpy as np
from jax import lax
from jax.sharding import Mesh
from jax.sharding import PartitionSpec as P

HEAD_DIM = 128
BLOCK = 128
REACH = 3
NEG_FILL = -1e30

CTX_PARTS = (("z", 8), ("x", 4), ("y_lo", 2))
TP_PARTS = (("y_hi", 2), ("core", 2))
CTX = tuple(name for name, _ in CTX_PARTS)
TP = tuple(name for name, _ in TP_PARTS)


def from_earlier(block, distance, count):
    route = [(i - distance, i) for i in range(count) if 0 <= i - distance < count]
    return lax.ppermute(block, CTX, route)


def to_earlier(block, distance, count):
    route = [(i, i - distance) for i in range(count) if 0 <= i - distance < count]
    return lax.ppermute(block, CTX, route)


def swapped(block, axis):
    return lax.ppermute(block, axis, [(0, 1), (1, 0)])


def in_order(own, other, place):
    first = jnp.where(place == 0, own, other)
    second = jnp.where(place == 0, other, own)
    return jnp.stack([first, second])


def gathered_over_tp(piece, after):
    high = lax.axis_index(TP[0])
    low = lax.axis_index(TP[1])
    other, after = lax.optimization_barrier((swapped(piece, TP[0]), after))
    by_high = in_order(piece, other, high)
    both = in_order(by_high, swapped(by_high, TP[1]), low)
    return jnp.transpose(both, (1, 0, 2, 3)).reshape(-1, piece.shape[1]), after


def summed_over_tp(part):
    high = lax.axis_index(TP[0])
    low = lax.axis_index(TP[1])
    quarters = part.reshape(2, 2, part.shape[0] // 4, part.shape[1])
    kept = lax.dynamic_index_in_dim(quarters, low, 1, keepdims=False)
    given = lax.dynamic_index_in_dim(quarters, 1 - low, 1, keepdims=False)
    halves = kept + swapped(given.astype(jnp.bfloat16), TP[1]).astype(jnp.float32)
    kept = lax.dynamic_index_in_dim(halves, high, 0, keepdims=False)
    given = lax.dynamic_index_in_dim(halves, 1 - high, 0, keepdims=False)
    return kept + swapped(given.astype(jnp.bfloat16), TP[0]).astype(jnp.float32)


def on_device(query_rows, key_rows, value_rows, out_weight, out_grad, doc_ids, window_blocks):
    tokens_here = query_rows.shape[0]
    kv_width = key_rows.shape[1]
    kv_here = kv_width // HEAD_DIM
    groups = query_rows.shape[1] // kv_width
    score_scale = HEAD_DIM ** (-0.5)
    ctx_count = lax.axis_size(CTX)
    ctx_place = lax.axis_index(CTX)
    my_start = ctx_place * tokens_here
    span = REACH * tokens_here
    key_count = span + tokens_here

    own_pair = jnp.concatenate([key_rows, value_rows], axis=1)
    earlier = [from_earlier(own_pair, distance, ctx_count) for distance in range(REACH, 0, -1)]
    pairs_all = jnp.concatenate(earlier + [own_pair], axis=0)
    keys_all = pairs_all[:, :kv_width]
    values_all = pairs_all[:, kv_width:]
    key_heads = keys_all.reshape(key_count, kv_here, HEAD_DIM)
    value_heads = values_all.reshape(key_count, kv_here, HEAD_DIM)

    doc_pad = jnp.concatenate([jnp.full((span,), -1, jnp.int32), doc_ids.astype(jnp.int32)])
    query_pos = my_start + jnp.arange(tokens_here, dtype=jnp.int32)
    key_pos = my_start - span + jnp.arange(key_count, dtype=jnp.int32)
    query_doc = lax.dynamic_slice_in_dim(doc_ids, my_start, tokens_here)
    key_doc = lax.dynamic_slice_in_dim(doc_pad, my_start, key_count)
    query_width = jnp.repeat(
        lax.dynamic_slice_in_dim(window_blocks, my_start // BLOCK, tokens_here // BLOCK), BLOCK
    )
    allowed = (
        (key_pos[None, :] >= 0)
        & (key_pos[None, :] <= query_pos[:, None])
        & (query_doc[:, None] == key_doc[None, :])
        & (query_pos[:, None] // BLOCK - key_pos[None, :] // BLOCK < query_width[:, None])
    )

    query_four = query_rows.reshape(tokens_here, kv_here, groups, HEAD_DIM)
    scores = (
        jnp.einsum("qcgd,kcd->cgqk", query_four, key_heads, preferred_element_type=jnp.float32)
        * score_scale
    )
    masked = jnp.where(allowed, scores, NEG_FILL)
    row_max = jnp.max(masked, axis=-1)
    expo = jnp.where(allowed, jnp.exp(masked - row_max[..., None]), 0.0)
    total = jnp.sum(expo, axis=-1)
    summed = jnp.einsum(
        "cgqk,kcd->qcgd", expo.astype(jnp.bfloat16), value_heads, preferred_element_type=jnp.float32
    )
    attn_four = summed / jnp.transpose(total, (2, 0, 1))[..., None]
    attn = attn_four.reshape(tokens_here, -1).astype(jnp.bfloat16)
    log_sum = row_max + jnp.log(total)
    grad_piece, attn = gathered_over_tp(out_grad, attn)

    weight_part = lax.dot_general(
        attn, grad_piece, (((0,), (0,)), ((), ())), preferred_element_type=jnp.float32
    ).astype(jnp.bfloat16)
    weight_part, attn, grad_piece = lax.optimization_barrier((weight_part, attn, grad_piece))
    weight_sum = lax.psum_scatter(weight_part, CTX[0], scatter_dimension=1, tiled=True)

    out_part = jnp.dot(attn, out_weight, preferred_element_type=jnp.float32)
    layer_out = summed_over_tp(out_part).astype(jnp.bfloat16)
    rest_count = ctx_count // lax.axis_size(CTX[0])
    weight_cols = weight_sum.reshape(weight_sum.shape[0], rest_count, -1).transpose(1, 0, 2)
    weight_cols = lax.all_to_all(weight_cols, CTX[1:], 0, 0, tiled=True)
    weight_sum = jnp.sum(weight_cols.astype(jnp.float32), axis=0)
    seq_total = ctx_count * tokens_here
    grad_weight = weight_sum * seq_total ** (-0.5)

    d_attn = lax.dot_general(
        grad_piece, out_weight, (((1,), (1,)), ((), ())), preferred_element_type=jnp.float32
    ).astype(jnp.bfloat16)
    grad_four = d_attn.reshape(tokens_here, kv_here, groups, HEAD_DIM)
    delta_rows = jnp.transpose(
        jnp.sum(
            grad_four.astype(jnp.float32)
            * attn.reshape(tokens_here, kv_here, groups, HEAD_DIM).astype(jnp.float32),
            axis=-1,
        ),
        (1, 2, 0),
    )

    probs = jnp.exp(jnp.where(allowed, scores - log_sum[..., None], NEG_FILL))
    d_probs = jnp.einsum(
        "qcgd,kcd->cgqk", grad_four, value_heads, preferred_element_type=jnp.float32
    )
    d_scores = (probs * (d_probs - delta_rows[..., None]) * score_scale).astype(jnp.bfloat16)
    probs_half = probs.astype(jnp.bfloat16)

    def key_side(score_part, prob_part):
        key_part = jnp.einsum(
            "cgqk,qcgd->kcd", score_part, query_four, preferred_element_type=jnp.float32
        )
        value_part = jnp.einsum(
            "cgqk,qcgd->kcd", prob_part, grad_four, preferred_element_type=jnp.float32
        )
        rows = score_part.shape[-1]
        return jnp.concatenate(
            [key_part.reshape(rows, kv_width), value_part.reshape(rows, kv_width)], axis=1
        )

    early_grad = key_side(d_scores[..., :span], probs_half[..., :span]).astype(jnp.bfloat16)
    early_grad, d_scores, probs_half = lax.optimization_barrier((early_grad, d_scores, probs_half))
    returned = []
    for distance in range(1, REACH + 1):
        lo = span - distance * tokens_here
        returned.append(to_earlier(early_grad[lo : lo + tokens_here], distance, ctx_count))
    query_grad = jnp.einsum(
        "cgqk,kcd->qcgd", d_scores, key_heads, preferred_element_type=jnp.float32
    )
    pair_grad = key_side(d_scores[..., span:], probs_half[..., span:])
    returned, grad_weight = lax.optimization_barrier((returned, grad_weight))
    for sent in returned:
        pair_grad = pair_grad + sent.astype(jnp.float32)
    key_grad = pair_grad[:, :kv_width]
    value_grad = pair_grad[:, kv_width:]

    grad_queries = query_grad.reshape(tokens_here, -1).astype(jnp.bfloat16)
    grad_keys = key_grad.astype(jnp.bfloat16)
    grad_values = value_grad.astype(jnp.bfloat16)
    return (layer_out, grad_queries, grad_keys, grad_values, grad_weight)


def solution(mesh):
    shape = tuple(size for _, size in CTX_PARTS + TP_PARTS)
    fine = Mesh(np.asarray(mesh.devices).reshape(shape), CTX + TP)
    placed = (
        P(CTX, TP),
        P(CTX, TP),
        P(CTX, TP),
        P(TP, None),
        P(CTX + TP, None),
        P(),
        P(),
    )
    return jax.shard_map(
        on_device,
        mesh=fine,
        in_specs=placed,
        out_specs=(
            P(CTX + TP, None),
            P(CTX, TP),
            P(CTX, TP),
            P(CTX, TP),
            P(TP, CTX),
        ),
        check_vma=False,
    )
```

```python
import jax
import jax.numpy as jnp
import numpy as np
from jax import lax
from jax.sharding import Mesh
from jax.sharding import PartitionSpec as P

HEAD_DIM = 128
BLOCK = 128
REACH = 3
NEG_FILL = -1e30

CTX_PARTS = (("z", 8), ("x", 4), ("y_lo", 2))
TP_PARTS = (("y_hi", 2), ("core", 2))
CTX = tuple(name for name, _ in CTX_PARTS)
TP = tuple(name for name, _ in TP_PARTS)


def from_earlier(block, distance, count):
    route = [(i - distance, i) for i in range(count) if 0 <= i - distance < count]
    return lax.ppermute(block, CTX, route)


def to_earlier(block, distance, count):
    route = [(i, i - distance) for i in range(count) if 0 <= i - distance < count]
    return lax.ppermute(block, CTX, route)


def swapped(block, axis):
    return lax.ppermute(block, axis, [(0, 1), (1, 0)])


def in_order(own, other, place):
    first = jnp.where(place == 0, own, other)
    second = jnp.where(place == 0, other, own)
    return jnp.stack([first, second])


def gathered_over_tp(piece, after):
    high = lax.axis_index(TP[0])
    low = lax.axis_index(TP[1])
    other, after = lax.optimization_barrier((swapped(piece, TP[0]), after))
    by_high = in_order(piece, other, high)
    both = in_order(by_high, swapped(by_high, TP[1]), low)
    return jnp.transpose(both, (1, 0, 2, 3)).reshape(-1, piece.shape[1]), after


def summed_over_tp(part, after):
    high = lax.axis_index(TP[0])
    low = lax.axis_index(TP[1])
    quarters = part.reshape(2, 2, part.shape[0] // 4, part.shape[1])
    kept = lax.dynamic_index_in_dim(quarters, low, 1, keepdims=False)
    given = lax.dynamic_index_in_dim(quarters, 1 - low, 1, keepdims=False)
    halves = kept + swapped(given.astype(jnp.bfloat16), TP[1]).astype(jnp.float32)
    halves, after = lax.optimization_barrier((halves, after))
    kept = lax.dynamic_index_in_dim(halves, high, 0, keepdims=False)
    given = lax.dynamic_index_in_dim(halves, 1 - high, 0, keepdims=False)
    return kept + swapped(given.astype(jnp.bfloat16), TP[0]).astype(jnp.float32), after


def on_device(query_rows, key_rows, value_rows, out_weight, out_grad, doc_ids, window_blocks):
    tokens_here = query_rows.shape[0]
    kv_width = key_rows.shape[1]
    kv_here = kv_width // HEAD_DIM
    groups = query_rows.shape[1] // kv_width
    score_scale = HEAD_DIM ** (-0.5)
    ctx_count = lax.axis_size(CTX)
    ctx_place = lax.axis_index(CTX)
    my_start = ctx_place * tokens_here
    span = REACH * tokens_here
    key_count = span + tokens_here

    own_pair = jnp.concatenate([key_rows, value_rows], axis=1)
    earlier = [from_earlier(own_pair, distance, ctx_count) for distance in range(REACH, 0, -1)]
    pairs_all = jnp.concatenate(earlier + [own_pair], axis=0)
    keys_all = pairs_all[:, :kv_width]
    values_all = pairs_all[:, kv_width:]
    key_heads = keys_all.reshape(key_count, kv_here, HEAD_DIM)
    value_heads = values_all.reshape(key_count, kv_here, HEAD_DIM)

    doc_pad = jnp.concatenate([jnp.full((span,), -1, jnp.int32), doc_ids.astype(jnp.int32)])
    query_pos = my_start + jnp.arange(tokens_here, dtype=jnp.int32)
    key_pos = my_start - span + jnp.arange(key_count, dtype=jnp.int32)
    query_doc = lax.dynamic_slice_in_dim(doc_ids, my_start, tokens_here)
    key_doc = lax.dynamic_slice_in_dim(doc_pad, my_start, key_count)
    query_width = jnp.repeat(
        lax.dynamic_slice_in_dim(window_blocks, my_start // BLOCK, tokens_here // BLOCK), BLOCK
    )
    allowed = (
        (key_pos[None, :] >= 0)
        & (key_pos[None, :] <= query_pos[:, None])
        & (query_doc[:, None] == key_doc[None, :])
        & (query_pos[:, None] // BLOCK - key_pos[None, :] // BLOCK < query_width[:, None])
    )

    query_four = query_rows.reshape(tokens_here, kv_here, groups, HEAD_DIM)
    scores = (
        jnp.einsum("qcgd,kcd->cgqk", query_four, key_heads, preferred_element_type=jnp.float32)
        * score_scale
    )
    masked = jnp.where(allowed, scores, NEG_FILL)
    row_max = jnp.max(masked, axis=-1)
    expo = jnp.where(allowed, jnp.exp(masked - row_max[..., None]), 0.0)
    total = jnp.sum(expo, axis=-1)
    summed = jnp.einsum(
        "cgqk,kcd->qcgd", expo.astype(jnp.bfloat16), value_heads, preferred_element_type=jnp.float32
    )
    attn_four = summed / jnp.transpose(total, (2, 0, 1))[..., None]
    attn = attn_four.reshape(tokens_here, -1).astype(jnp.bfloat16)
    log_sum = row_max + jnp.log(total)
    grad_piece, attn = gathered_over_tp(out_grad, attn)

    weight_part = lax.dot_general(
        attn, grad_piece, (((0,), (0,)), ((), ())), preferred_element_type=jnp.float32
    ).astype(jnp.bfloat16)
    weight_part, attn, grad_piece = lax.optimization_barrier((weight_part, attn, grad_piece))
    weight_sum = lax.psum_scatter(weight_part, CTX[0], scatter_dimension=1, tiled=True)

    out_part = jnp.dot(attn, out_weight, preferred_element_type=jnp.float32)
    rest_count = ctx_count // lax.axis_size(CTX[0])
    weight_cols = weight_sum.reshape(weight_sum.shape[0], rest_count, -1).transpose(1, 0, 2)
    weight_cols = lax.all_to_all(weight_cols, CTX[1:], 0, 0, tiled=True)
    weight_sum = jnp.sum(weight_cols.astype(jnp.float32), axis=0)
    seq_total = ctx_count * tokens_here
    grad_weight = weight_sum * seq_total ** (-0.5)

    d_attn = lax.dot_general(
        grad_piece, out_weight, (((1,), (1,)), ((), ())), preferred_element_type=jnp.float32
    ).astype(jnp.bfloat16)
    layer_sum, d_attn = summed_over_tp(out_part, d_attn)
    layer_out = layer_sum.astype(jnp.bfloat16)
    grad_four = d_attn.reshape(tokens_here, kv_here, groups, HEAD_DIM)
    delta_rows = jnp.transpose(
        jnp.sum(
            grad_four.astype(jnp.float32)
            * attn.reshape(tokens_here, kv_here, groups, HEAD_DIM).astype(jnp.float32),
            axis=-1,
        ),
        (1, 2, 0),
    )

    probs = jnp.exp(jnp.where(allowed, scores - log_sum[..., None], NEG_FILL))
    d_probs = jnp.einsum(
        "qcgd,kcd->cgqk", grad_four, value_heads, preferred_element_type=jnp.float32
    )
    d_scores = (probs * (d_probs - delta_rows[..., None]) * score_scale).astype(jnp.bfloat16)
    probs_half = probs.astype(jnp.bfloat16)

    def key_side(score_part, prob_part):
        key_part = jnp.einsum(
            "cgqk,qcgd->kcd", score_part, query_four, preferred_element_type=jnp.float32
        )
        value_part = jnp.einsum(
            "cgqk,qcgd->kcd", prob_part, grad_four, preferred_element_type=jnp.float32
        )
        rows = score_part.shape[-1]
        return jnp.concatenate(
            [key_part.reshape(rows, kv_width), value_part.reshape(rows, kv_width)], axis=1
        )

    early_grad = key_side(d_scores[..., :span], probs_half[..., :span]).astype(jnp.bfloat16)
    early_grad, d_scores, probs_half = lax.optimization_barrier((early_grad, d_scores, probs_half))
    returned = []
    for distance in range(1, REACH + 1):
        lo = span - distance * tokens_here
        returned.append(to_earlier(early_grad[lo : lo + tokens_here], distance, ctx_count))
    query_grad = jnp.einsum(
        "cgqk,kcd->qcgd", d_scores, key_heads, preferred_element_type=jnp.float32
    )
    pair_grad = key_side(d_scores[..., span:], probs_half[..., span:])
    returned, grad_weight = lax.optimization_barrier((returned, grad_weight))
    for sent in returned:
        pair_grad = pair_grad + sent.astype(jnp.float32)
    key_grad = pair_grad[:, :kv_width]
    value_grad = pair_grad[:, kv_width:]

    grad_queries = query_grad.reshape(tokens_here, -1).astype(jnp.bfloat16)
    grad_keys = key_grad.astype(jnp.bfloat16)
    grad_values = value_grad.astype(jnp.bfloat16)
    return (layer_out, grad_queries, grad_keys, grad_values, grad_weight)


def solution(mesh):
    shape = tuple(size for _, size in CTX_PARTS + TP_PARTS)
    fine = Mesh(np.asarray(mesh.devices).reshape(shape), CTX + TP)
    placed = (
        P(CTX, TP),
        P(CTX, TP),
        P(CTX, TP),
        P(TP, None),
        P(CTX + TP, None),
        P(),
        P(),
    )
    return jax.shard_map(
        on_device,
        mesh=fine,
        in_specs=placed,
        out_specs=(
            P(CTX + TP, None),
            P(CTX, TP),
            P(CTX, TP),
            P(CTX, TP),
            P(TP, CTX),
        ),
        check_vma=False,
    )
```

```python
import jax
import jax.numpy as jnp
import numpy as np
from jax import lax
from jax.sharding import Mesh
from jax.sharding import PartitionSpec as P

HEAD_DIM = 128
BLOCK = 128
REACH = 3
NEG_FILL = -1e30

CTX_PARTS = (("z", 8), ("x", 4), ("y_lo", 2))
TP_PARTS = (("y_hi", 2), ("core", 2))
CTX = tuple(name for name, _ in CTX_PARTS)
TP = tuple(name for name, _ in TP_PARTS)


def from_earlier(block, distance, count):
    route = [(i - distance, i) for i in range(count) if 0 <= i - distance < count]
    return lax.ppermute(block, CTX, route)


def to_earlier(block, distance, count):
    route = [(i, i - distance) for i in range(count) if 0 <= i - distance < count]
    return lax.ppermute(block, CTX, route)


def swapped(block, axis):
    return lax.ppermute(block, axis, [(0, 1), (1, 0)])


def in_order(own, other, place):
    first = jnp.where(place == 0, own, other)
    second = jnp.where(place == 0, other, own)
    return jnp.stack([first, second])


def gathered_over_tp(piece, after):
    high = lax.axis_index(TP[0])
    low = lax.axis_index(TP[1])
    other, after = lax.optimization_barrier((swapped(piece, TP[0]), after))
    by_high = in_order(piece, other, high)
    both = in_order(by_high, swapped(by_high, TP[1]), low)
    return jnp.transpose(both, (1, 0, 2, 3)).reshape(-1, piece.shape[1]), after


def summed_over_tp(part):
    high = lax.axis_index(TP[0])
    low = lax.axis_index(TP[1])
    quarters = part.reshape(2, 2, part.shape[0] // 4, part.shape[1])
    kept = lax.dynamic_index_in_dim(quarters, low, 1, keepdims=False)
    given = lax.dynamic_index_in_dim(quarters, 1 - low, 1, keepdims=False)
    halves = kept + swapped(given.astype(jnp.bfloat16), TP[1]).astype(jnp.float32)
    kept = lax.dynamic_index_in_dim(halves, high, 0, keepdims=False)
    given = lax.dynamic_index_in_dim(halves, 1 - high, 0, keepdims=False)
    return kept, swapped(given.astype(jnp.bfloat16), TP[0])


def on_device(query_rows, key_rows, value_rows, out_weight, out_grad, doc_ids, window_blocks):
    tokens_here = query_rows.shape[0]
    kv_width = key_rows.shape[1]
    kv_here = kv_width // HEAD_DIM
    groups = query_rows.shape[1] // kv_width
    score_scale = HEAD_DIM ** (-0.5)
    ctx_count = lax.axis_size(CTX)
    ctx_place = lax.axis_index(CTX)
    my_start = ctx_place * tokens_here
    span = REACH * tokens_here
    key_count = span + tokens_here

    own_pair = jnp.concatenate([key_rows, value_rows], axis=1)
    earlier = [from_earlier(own_pair, distance, ctx_count) for distance in range(REACH, 0, -1)]
    pairs_all = jnp.concatenate(earlier + [own_pair], axis=0)
    keys_all = pairs_all[:, :kv_width]
    values_all = pairs_all[:, kv_width:]
    key_heads = keys_all.reshape(key_count, kv_here, HEAD_DIM)
    value_heads = values_all.reshape(key_count, kv_here, HEAD_DIM)

    doc_pad = jnp.concatenate([jnp.full((span,), -1, jnp.int32), doc_ids.astype(jnp.int32)])
    query_pos = my_start + jnp.arange(tokens_here, dtype=jnp.int32)
    key_pos = my_start - span + jnp.arange(key_count, dtype=jnp.int32)
    query_doc = lax.dynamic_slice_in_dim(doc_ids, my_start, tokens_here)
    key_doc = lax.dynamic_slice_in_dim(doc_pad, my_start, key_count)
    query_width = jnp.repeat(
        lax.dynamic_slice_in_dim(window_blocks, my_start // BLOCK, tokens_here // BLOCK), BLOCK
    )
    allowed = (
        (key_pos[None, :] >= 0)
        & (key_pos[None, :] <= query_pos[:, None])
        & (query_doc[:, None] == key_doc[None, :])
        & (query_pos[:, None] // BLOCK - key_pos[None, :] // BLOCK < query_width[:, None])
    )

    query_four = query_rows.reshape(tokens_here, kv_here, groups, HEAD_DIM)
    scores = (
        jnp.einsum("qcgd,kcd->cgqk", query_four, key_heads, preferred_element_type=jnp.float32)
        * score_scale
    )
    masked = jnp.where(allowed, scores, NEG_FILL)
    row_max = jnp.max(masked, axis=-1)
    expo = jnp.where(allowed, jnp.exp(masked - row_max[..., None]), 0.0)
    total = jnp.sum(expo, axis=-1)
    summed = jnp.einsum(
        "cgqk,kcd->qcgd", expo.astype(jnp.bfloat16), value_heads, preferred_element_type=jnp.float32
    )
    attn_four = summed / jnp.transpose(total, (2, 0, 1))[..., None]
    attn = attn_four.reshape(tokens_here, -1).astype(jnp.bfloat16)
    log_sum = row_max + jnp.log(total)
    grad_piece, attn = gathered_over_tp(out_grad, attn)

    weight_part = lax.dot_general(
        attn, grad_piece, (((0,), (0,)), ((), ())), preferred_element_type=jnp.float32
    ).astype(jnp.bfloat16)
    weight_part, attn, grad_piece = lax.optimization_barrier((weight_part, attn, grad_piece))
    weight_sum = lax.psum_scatter(weight_part, CTX[0], scatter_dimension=1, tiled=True)

    out_part = jnp.dot(attn, out_weight, preferred_element_type=jnp.float32)
    layer_kept, layer_received = summed_over_tp(out_part)
    rest_count = ctx_count // lax.axis_size(CTX[0])
    weight_cols = weight_sum.reshape(weight_sum.shape[0], rest_count, -1).transpose(1, 0, 2)
    weight_cols = lax.all_to_all(weight_cols, CTX[1:], 0, 0, tiled=True)
    weight_sum = jnp.sum(weight_cols.astype(jnp.float32), axis=0)
    seq_total = ctx_count * tokens_here
    grad_weight = weight_sum * seq_total ** (-0.5)

    d_attn = lax.dot_general(
        grad_piece, out_weight, (((1,), (1,)), ((), ())), preferred_element_type=jnp.float32
    ).astype(jnp.bfloat16)
    grad_four = d_attn.reshape(tokens_here, kv_here, groups, HEAD_DIM)
    delta_rows = jnp.transpose(
        jnp.sum(
            grad_four.astype(jnp.float32)
            * attn.reshape(tokens_here, kv_here, groups, HEAD_DIM).astype(jnp.float32),
            axis=-1,
        ),
        (1, 2, 0),
    )

    probs = jnp.exp(jnp.where(allowed, scores - log_sum[..., None], NEG_FILL))
    d_probs = jnp.einsum(
        "qcgd,kcd->cgqk", grad_four, value_heads, preferred_element_type=jnp.float32
    )
    d_scores = (probs * (d_probs - delta_rows[..., None]) * score_scale).astype(jnp.bfloat16)
    probs_half = probs.astype(jnp.bfloat16)

    def key_side(score_part, prob_part):
        key_part = jnp.einsum(
            "cgqk,qcgd->kcd", score_part, query_four, preferred_element_type=jnp.float32
        )
        value_part = jnp.einsum(
            "cgqk,qcgd->kcd", prob_part, grad_four, preferred_element_type=jnp.float32
        )
        rows = score_part.shape[-1]
        return jnp.concatenate(
            [key_part.reshape(rows, kv_width), value_part.reshape(rows, kv_width)], axis=1
        )

    early_grad = key_side(d_scores[..., :span], probs_half[..., :span]).astype(jnp.bfloat16)
    early_grad, d_scores, probs_half = lax.optimization_barrier((early_grad, d_scores, probs_half))
    returned = []
    for distance in range(1, REACH + 1):
        lo = span - distance * tokens_here
        returned.append(to_earlier(early_grad[lo : lo + tokens_here], distance, ctx_count))
    query_grad = jnp.einsum(
        "cgqk,kcd->qcgd", d_scores, key_heads, preferred_element_type=jnp.float32
    )
    pair_grad = key_side(d_scores[..., span:], probs_half[..., span:])
    returned, grad_weight, layer_received = lax.optimization_barrier(
        (returned, grad_weight, layer_received)
    )
    layer_out = (layer_kept + layer_received.astype(jnp.float32)).astype(jnp.bfloat16)
    for sent in returned:
        pair_grad = pair_grad + sent.astype(jnp.float32)
    key_grad = pair_grad[:, :kv_width]
    value_grad = pair_grad[:, kv_width:]

    grad_queries = query_grad.reshape(tokens_here, -1).astype(jnp.bfloat16)
    grad_keys = key_grad.astype(jnp.bfloat16)
    grad_values = value_grad.astype(jnp.bfloat16)
    return (layer_out, grad_queries, grad_keys, grad_values, grad_weight)


def solution(mesh):
    shape = tuple(size for _, size in CTX_PARTS + TP_PARTS)
    fine = Mesh(np.asarray(mesh.devices).reshape(shape), CTX + TP)
    placed = (
        P(CTX, TP),
        P(CTX, TP),
        P(CTX, TP),
        P(TP, None),
        P(CTX + TP, None),
        P(),
        P(),
    )
    return jax.shard_map(
        on_device,
        mesh=fine,
        in_specs=placed,
        out_specs=(
            P(CTX + TP, None),
            P(CTX, TP),
            P(CTX, TP),
            P(CTX, TP),
            P(TP, CTX),
        ),
        check_vma=False,
    )
```

```python
import jax
import jax.numpy as jnp
import numpy as np
from jax import lax
from jax.sharding import Mesh
from jax.sharding import PartitionSpec as P

HEAD_DIM = 128
BLOCK = 128
REACH = 3
NEG_FILL = -1e30

CTX_PARTS = (("z", 8), ("x", 4), ("y_lo", 2))
TP_PARTS = (("y_hi", 2), ("core", 2))
CTX = tuple(name for name, _ in CTX_PARTS)
TP = tuple(name for name, _ in TP_PARTS)


def from_earlier(block, distance, count):
    route = [(i - distance, i) for i in range(count) if 0 <= i - distance < count]
    return lax.ppermute(block, CTX, route)


def to_earlier(block, distance, count):
    route = [(i, i - distance) for i in range(count) if 0 <= i - distance < count]
    return lax.ppermute(block, CTX, route)


def swapped(block, axis):
    return lax.ppermute(block, axis, [(0, 1), (1, 0)])


def in_order(own, other, place):
    first = jnp.where(place == 0, own, other)
    second = jnp.where(place == 0, other, own)
    return jnp.stack([first, second])


def gathered_over_tp(piece, after):
    high = lax.axis_index(TP[0])
    low = lax.axis_index(TP[1])
    other, after = lax.optimization_barrier((swapped(piece, TP[0]), after))
    by_high = in_order(piece, other, high)
    both = in_order(by_high, swapped(by_high, TP[1]), low)
    return jnp.transpose(both, (1, 0, 2, 3)).reshape(-1, piece.shape[1]), after


def summed_over_tp(part):
    high = lax.axis_index(TP[0])
    low = lax.axis_index(TP[1])
    quarters = part.reshape(2, 2, part.shape[0] // 4, part.shape[1])
    kept = lax.dynamic_index_in_dim(quarters, low, 1, keepdims=False)
    given = lax.dynamic_index_in_dim(quarters, 1 - low, 1, keepdims=False)
    halves = kept + swapped(given.astype(jnp.bfloat16), TP[1]).astype(jnp.float32)
    kept = lax.dynamic_index_in_dim(halves, high, 0, keepdims=False)
    given = lax.dynamic_index_in_dim(halves, 1 - high, 0, keepdims=False)
    return kept + swapped(given.astype(jnp.bfloat16), TP[0]).astype(jnp.float32)


def on_device(query_rows, key_rows, value_rows, out_weight, out_grad, doc_ids, window_blocks):
    tokens_here = query_rows.shape[0]
    kv_width = key_rows.shape[1]
    kv_here = kv_width // HEAD_DIM
    groups = query_rows.shape[1] // kv_width
    score_scale = HEAD_DIM ** (-0.5)
    ctx_count = lax.axis_size(CTX)
    ctx_place = lax.axis_index(CTX)
    my_start = ctx_place * tokens_here
    span = REACH * tokens_here
    key_count = span + tokens_here

    own_pair = jnp.concatenate([key_rows, value_rows], axis=1)
    earlier = [from_earlier(own_pair, distance, ctx_count) for distance in range(REACH, 0, -1)]
    pairs_all = jnp.concatenate(earlier + [own_pair], axis=0)
    keys_all = pairs_all[:, :kv_width]
    values_all = pairs_all[:, kv_width:]
    key_heads = keys_all.reshape(key_count, kv_here, HEAD_DIM)
    value_heads = values_all.reshape(key_count, kv_here, HEAD_DIM)

    doc_pad = jnp.concatenate([jnp.full((span,), -1, jnp.int32), doc_ids.astype(jnp.int32)])
    query_pos = my_start + jnp.arange(tokens_here, dtype=jnp.int32)
    key_pos = my_start - span + jnp.arange(key_count, dtype=jnp.int32)
    query_doc = lax.dynamic_slice_in_dim(doc_ids, my_start, tokens_here)
    key_doc = lax.dynamic_slice_in_dim(doc_pad, my_start, key_count)
    query_width = jnp.repeat(
        lax.dynamic_slice_in_dim(window_blocks, my_start // BLOCK, tokens_here // BLOCK), BLOCK
    )
    allowed = (
        (key_pos[None, :] >= 0)
        & (key_pos[None, :] <= query_pos[:, None])
        & (query_doc[:, None] == key_doc[None, :])
        & (query_pos[:, None] // BLOCK - key_pos[None, :] // BLOCK < query_width[:, None])
    )

    query_four = query_rows.reshape(tokens_here, kv_here, groups, HEAD_DIM)
    scores = (
        jnp.einsum("qcgd,kcd->cgqk", query_four, key_heads, preferred_element_type=jnp.float32)
        * score_scale
    )
    masked = jnp.where(allowed, scores, NEG_FILL)
    row_max = jnp.max(masked, axis=-1)
    expo = jnp.where(allowed, jnp.exp(masked - row_max[..., None]), 0.0)
    total = jnp.sum(expo, axis=-1)
    summed = jnp.einsum(
        "cgqk,kcd->qcgd", expo.astype(jnp.bfloat16), value_heads, preferred_element_type=jnp.float32
    )
    attn_four = summed / jnp.transpose(total, (2, 0, 1))[..., None]
    attn = attn_four.reshape(tokens_here, -1).astype(jnp.bfloat16)
    log_sum = row_max + jnp.log(total)
    grad_piece, attn = gathered_over_tp(out_grad, attn)

    weight_part = lax.dot_general(
        grad_piece, attn, (((0,), (0,)), ((), ())), preferred_element_type=jnp.float32
    ).astype(jnp.bfloat16)
    weight_part, attn, grad_piece = lax.optimization_barrier((weight_part, attn, grad_piece))
    weight_sum = lax.psum_scatter(weight_part, CTX[0], scatter_dimension=0, tiled=True)

    out_part = jnp.dot(attn, out_weight, preferred_element_type=jnp.float32)
    layer_out = summed_over_tp(out_part).astype(jnp.bfloat16)
    rest_count = ctx_count // lax.axis_size(CTX[0])
    weight_cols = weight_sum.reshape(rest_count, -1, weight_sum.shape[1])
    weight_cols = lax.all_to_all(weight_cols, CTX[1:], 0, 0, tiled=True)
    weight_sum = jnp.sum(weight_cols.astype(jnp.float32), axis=0).T
    seq_total = ctx_count * tokens_here
    grad_weight = weight_sum * seq_total ** (-0.5)

    d_attn = lax.dot_general(
        grad_piece, out_weight, (((1,), (1,)), ((), ())), preferred_element_type=jnp.float32
    ).astype(jnp.bfloat16)
    grad_four = d_attn.reshape(tokens_here, kv_here, groups, HEAD_DIM)
    delta_rows = jnp.transpose(
        jnp.sum(
            grad_four.astype(jnp.float32)
            * attn.reshape(tokens_here, kv_here, groups, HEAD_DIM).astype(jnp.float32),
            axis=-1,
        ),
        (1, 2, 0),
    )

    probs = jnp.exp(jnp.where(allowed, scores - log_sum[..., None], NEG_FILL))
    d_probs = jnp.einsum(
        "qcgd,kcd->cgqk", grad_four, value_heads, preferred_element_type=jnp.float32
    )
    d_scores = (probs * (d_probs - delta_rows[..., None]) * score_scale).astype(jnp.bfloat16)
    probs_half = probs.astype(jnp.bfloat16)

    def key_side(score_part, prob_part):
        key_part = jnp.einsum(
            "cgqk,qcgd->kcd", score_part, query_four, preferred_element_type=jnp.float32
        )
        value_part = jnp.einsum(
            "cgqk,qcgd->kcd", prob_part, grad_four, preferred_element_type=jnp.float32
        )
        rows = score_part.shape[-1]
        return jnp.concatenate(
            [key_part.reshape(rows, kv_width), value_part.reshape(rows, kv_width)], axis=1
        )

    early_grad = key_side(d_scores[..., :span], probs_half[..., :span]).astype(jnp.bfloat16)
    early_grad, d_scores, probs_half = lax.optimization_barrier((early_grad, d_scores, probs_half))
    returned = []
    for distance in range(1, REACH + 1):
        lo = span - distance * tokens_here
        returned.append(to_earlier(early_grad[lo : lo + tokens_here], distance, ctx_count))
    query_grad = jnp.einsum(
        "cgqk,kcd->qcgd", d_scores, key_heads, preferred_element_type=jnp.float32
    )
    pair_grad = key_side(d_scores[..., span:], probs_half[..., span:])
    returned, grad_weight = lax.optimization_barrier((returned, grad_weight))
    for sent in returned:
        pair_grad = pair_grad + sent.astype(jnp.float32)
    key_grad = pair_grad[:, :kv_width]
    value_grad = pair_grad[:, kv_width:]

    grad_queries = query_grad.reshape(tokens_here, -1).astype(jnp.bfloat16)
    grad_keys = key_grad.astype(jnp.bfloat16)
    grad_values = value_grad.astype(jnp.bfloat16)
    return (layer_out, grad_queries, grad_keys, grad_values, grad_weight)


def solution(mesh):
    shape = tuple(size for _, size in CTX_PARTS + TP_PARTS)
    fine = Mesh(np.asarray(mesh.devices).reshape(shape), CTX + TP)
    placed = (
        P(CTX, TP),
        P(CTX, TP),
        P(CTX, TP),
        P(TP, None),
        P(CTX + TP, None),
        P(),
        P(),
    )
    return jax.shard_map(
        on_device,
        mesh=fine,
        in_specs=placed,
        out_specs=(
            P(CTX + TP, None),
            P(CTX, TP),
            P(CTX, TP),
            P(CTX, TP),
            P(TP, CTX),
        ),
        check_vma=False,
    )
```

```python
import jax
import jax.numpy as jnp
import numpy as np
from jax import lax
from jax.sharding import Mesh
from jax.sharding import PartitionSpec as P

HEAD_DIM = 128
BLOCK = 128
REACH = 3
NEG_FILL = -1e30

CTX_PARTS = (("z", 8), ("x", 4), ("y_lo", 2))
TP_PARTS = (("y_hi", 2), ("core", 2))
CTX = tuple(name for name, _ in CTX_PARTS)
TP = tuple(name for name, _ in TP_PARTS)


def from_earlier(block, distance, count):
    route = [(i - distance, i) for i in range(count) if 0 <= i - distance < count]
    return lax.ppermute(block, CTX, route)


def to_earlier(block, distance, count):
    route = [(i, i - distance) for i in range(count) if 0 <= i - distance < count]
    return lax.ppermute(block, CTX, route)


def swapped(block, axis):
    return lax.ppermute(block, axis, [(0, 1), (1, 0)])


def in_order(own, other, place):
    first = jnp.where(place == 0, own, other)
    second = jnp.where(place == 0, other, own)
    return jnp.stack([first, second])


def gathered_over_tp(piece, after):
    high = lax.axis_index(TP[0])
    low = lax.axis_index(TP[1])
    other, after = lax.optimization_barrier((swapped(piece, TP[0]), after))
    by_high = in_order(piece, other, high)
    partner = swapped(by_high, TP[1])
    both = in_order(by_high, partner, low)
    return jnp.transpose(both, (1, 0, 2, 3)).reshape(-1, piece.shape[1]), after, by_high, partner


def summed_over_tp(part):
    high = lax.axis_index(TP[0])
    low = lax.axis_index(TP[1])
    quarters = part.reshape(2, 2, part.shape[0] // 4, part.shape[1])
    kept = lax.dynamic_index_in_dim(quarters, low, 1, keepdims=False)
    given = lax.dynamic_index_in_dim(quarters, 1 - low, 1, keepdims=False)
    halves = kept + swapped(given.astype(jnp.bfloat16), TP[1]).astype(jnp.float32)
    kept = lax.dynamic_index_in_dim(halves, high, 0, keepdims=False)
    given = lax.dynamic_index_in_dim(halves, 1 - high, 0, keepdims=False)
    return kept + swapped(given.astype(jnp.bfloat16), TP[0]).astype(jnp.float32)


def on_device(query_rows, key_rows, value_rows, out_weight, out_grad, doc_ids, window_blocks):
    tokens_here = query_rows.shape[0]
    kv_width = key_rows.shape[1]
    kv_here = kv_width // HEAD_DIM
    groups = query_rows.shape[1] // kv_width
    score_scale = HEAD_DIM ** (-0.5)
    ctx_count = lax.axis_size(CTX)
    ctx_place = lax.axis_index(CTX)
    my_start = ctx_place * tokens_here
    span = REACH * tokens_here
    key_count = span + tokens_here

    own_pair = jnp.concatenate([key_rows, value_rows], axis=1)
    earlier = [from_earlier(own_pair, distance, ctx_count) for distance in range(REACH, 0, -1)]
    pairs_all = jnp.concatenate(earlier + [own_pair], axis=0)
    keys_all = pairs_all[:, :kv_width]
    values_all = pairs_all[:, kv_width:]
    key_heads = keys_all.reshape(key_count, kv_here, HEAD_DIM)
    value_heads = values_all.reshape(key_count, kv_here, HEAD_DIM)

    doc_pad = jnp.concatenate([jnp.full((span,), -1, jnp.int32), doc_ids.astype(jnp.int32)])
    query_pos = my_start + jnp.arange(tokens_here, dtype=jnp.int32)
    key_pos = my_start - span + jnp.arange(key_count, dtype=jnp.int32)
    query_doc = lax.dynamic_slice_in_dim(doc_ids, my_start, tokens_here)
    key_doc = lax.dynamic_slice_in_dim(doc_pad, my_start, key_count)
    query_width = jnp.repeat(
        lax.dynamic_slice_in_dim(window_blocks, my_start // BLOCK, tokens_here // BLOCK), BLOCK
    )
    allowed = (
        (key_pos[None, :] >= 0)
        & (key_pos[None, :] <= query_pos[:, None])
        & (query_doc[:, None] == key_doc[None, :])
        & (query_pos[:, None] // BLOCK - key_pos[None, :] // BLOCK < query_width[:, None])
    )

    query_four = query_rows.reshape(tokens_here, kv_here, groups, HEAD_DIM)
    scores = (
        jnp.einsum("qcgd,kcd->cgqk", query_four, key_heads, preferred_element_type=jnp.float32)
        * score_scale
    )
    masked = jnp.where(allowed, scores, NEG_FILL)
    row_max = jnp.max(masked, axis=-1)
    expo = jnp.where(allowed, jnp.exp(masked - row_max[..., None]), 0.0)
    total = jnp.sum(expo, axis=-1)
    summed = jnp.einsum(
        "cgqk,kcd->qcgd", expo.astype(jnp.bfloat16), value_heads, preferred_element_type=jnp.float32
    )
    attn_four = summed / jnp.transpose(total, (2, 0, 1))[..., None]
    attn = attn_four.reshape(tokens_here, -1).astype(jnp.bfloat16)
    log_sum = row_max + jnp.log(total)
    grad_piece, attn, own_rows, partner_rows = gathered_over_tp(out_grad, attn)
    low = lax.axis_index(TP[1])
    attn_quarters = attn.reshape(2, 2, tokens_here // 4, attn.shape[1])
    own_attn = lax.dynamic_index_in_dim(attn_quarters, low, 1, keepdims=False)
    partner_attn = lax.dynamic_index_in_dim(attn_quarters, 1 - low, 1, keepdims=False)
    contract = (((0, 1), (0, 1)), ((), ()))
    weight_part = lax.dot_general(
        own_rows, own_attn, contract, preferred_element_type=jnp.float32
    ) + lax.dot_general(partner_rows, partner_attn, contract, preferred_element_type=jnp.float32)
    weight_part = weight_part.astype(jnp.bfloat16)
    weight_part, attn, grad_piece = lax.optimization_barrier((weight_part, attn, grad_piece))
    weight_sum = lax.psum_scatter(weight_part, CTX[0], scatter_dimension=0, tiled=True)

    out_part = jnp.dot(attn, out_weight, preferred_element_type=jnp.float32)
    layer_out = summed_over_tp(out_part).astype(jnp.bfloat16)
    rest_count = ctx_count // lax.axis_size(CTX[0])
    weight_cols = weight_sum.reshape(rest_count, -1, weight_sum.shape[1])
    weight_cols = lax.all_to_all(weight_cols, CTX[1:], 0, 0, tiled=True)
    weight_sum = jnp.sum(weight_cols.astype(jnp.float32), axis=0).T
    seq_total = ctx_count * tokens_here
    grad_weight = weight_sum * seq_total ** (-0.5)

    d_attn = lax.dot_general(
        grad_piece, out_weight, (((1,), (1,)), ((), ())), preferred_element_type=jnp.float32
    ).astype(jnp.bfloat16)
    grad_four = d_attn.reshape(tokens_here, kv_here, groups, HEAD_DIM)
    delta_rows = jnp.transpose(
        jnp.sum(
            grad_four.astype(jnp.float32)
            * attn.reshape(tokens_here, kv_here, groups, HEAD_DIM).astype(jnp.float32),
            axis=-1,
        ),
        (1, 2, 0),
    )

    probs = jnp.exp(jnp.where(allowed, scores - log_sum[..., None], NEG_FILL))
    d_probs = jnp.einsum(
        "qcgd,kcd->cgqk", grad_four, value_heads, preferred_element_type=jnp.float32
    )
    d_scores = (probs * (d_probs - delta_rows[..., None]) * score_scale).astype(jnp.bfloat16)
    probs_half = probs.astype(jnp.bfloat16)

    def key_side(score_part, prob_part):
        key_part = jnp.einsum(
            "cgqk,qcgd->kcd", score_part, query_four, preferred_element_type=jnp.float32
        )
        value_part = jnp.einsum(
            "cgqk,qcgd->kcd", prob_part, grad_four, preferred_element_type=jnp.float32
        )
        rows = score_part.shape[-1]
        return jnp.concatenate(
            [key_part.reshape(rows, kv_width), value_part.reshape(rows, kv_width)], axis=1
        )

    early_grad = key_side(d_scores[..., :span], probs_half[..., :span]).astype(jnp.bfloat16)
    early_grad, d_scores, probs_half = lax.optimization_barrier((early_grad, d_scores, probs_half))
    returned = []
    for distance in range(1, REACH + 1):
        lo = span - distance * tokens_here
        returned.append(to_earlier(early_grad[lo : lo + tokens_here], distance, ctx_count))
    query_grad = jnp.einsum(
        "cgqk,kcd->qcgd", d_scores, key_heads, preferred_element_type=jnp.float32
    )
    pair_grad = key_side(d_scores[..., span:], probs_half[..., span:])
    returned, grad_weight = lax.optimization_barrier((returned, grad_weight))
    for sent in returned:
        pair_grad = pair_grad + sent.astype(jnp.float32)
    key_grad = pair_grad[:, :kv_width]
    value_grad = pair_grad[:, kv_width:]

    grad_queries = query_grad.reshape(tokens_here, -1).astype(jnp.bfloat16)
    grad_keys = key_grad.astype(jnp.bfloat16)
    grad_values = value_grad.astype(jnp.bfloat16)
    return (layer_out, grad_queries, grad_keys, grad_values, grad_weight)


def solution(mesh):
    shape = tuple(size for _, size in CTX_PARTS + TP_PARTS)
    fine = Mesh(np.asarray(mesh.devices).reshape(shape), CTX + TP)
    placed = (
        P(CTX, TP),
        P(CTX, TP),
        P(CTX, TP),
        P(TP, None),
        P(CTX + TP, None),
        P(),
        P(),
    )
    return jax.shard_map(
        on_device,
        mesh=fine,
        in_specs=placed,
        out_specs=(
            P(CTX + TP, None),
            P(CTX, TP),
            P(CTX, TP),
            P(CTX, TP),
            P(TP, CTX),
        ),
        check_vma=False,
    )
```

```python
import jax
import jax.numpy as jnp
import numpy as np
from jax import lax
from jax.sharding import Mesh
from jax.sharding import PartitionSpec as P

HEAD_DIM = 128
BLOCK = 128
REACH = 3
NEG_FILL = -1e30

CTX_PARTS = (("z", 8), ("x", 4), ("y_lo", 2))
TP_PARTS = (("y_hi", 2), ("core", 2))
CTX = tuple(name for name, _ in CTX_PARTS)
TP = tuple(name for name, _ in TP_PARTS)


def from_earlier(block, distance, count):
    route = [(i - distance, i) for i in range(count) if 0 <= i - distance < count]
    return lax.ppermute(block, CTX, route)


def to_earlier(block, distance, count):
    route = [(i, i - distance) for i in range(count) if 0 <= i - distance < count]
    return lax.ppermute(block, CTX, route)


def swapped(block, axis):
    return lax.ppermute(block, axis, [(0, 1), (1, 0)])


def in_order(own, other, place):
    first = jnp.where(place == 0, own, other)
    second = jnp.where(place == 0, other, own)
    return jnp.stack([first, second])


def gathered_over_tp(piece, after):
    high = lax.axis_index(TP[0])
    low = lax.axis_index(TP[1])
    other, after = lax.optimization_barrier((swapped(piece, TP[0]), after))
    by_high = in_order(piece, other, high)
    both = in_order(by_high, swapped(by_high, TP[1]), low)
    return jnp.transpose(both, (1, 0, 2, 3)).reshape(-1, piece.shape[1]), after


def summed_over_tp(part):
    high = lax.axis_index(TP[0])
    low = lax.axis_index(TP[1])
    quarters = part.reshape(2, 2, part.shape[0] // 4, part.shape[1])
    kept = lax.dynamic_index_in_dim(quarters, low, 1, keepdims=False)
    given = lax.dynamic_index_in_dim(quarters, 1 - low, 1, keepdims=False)
    halves = kept + swapped(given.astype(jnp.bfloat16), TP[1]).astype(jnp.float32)
    kept = lax.dynamic_index_in_dim(halves, high, 0, keepdims=False)
    given = lax.dynamic_index_in_dim(halves, 1 - high, 0, keepdims=False)
    return kept + swapped(given.astype(jnp.bfloat16), TP[0]).astype(jnp.float32)


def on_device(query_rows, key_rows, value_rows, out_weight, out_grad, doc_ids, window_blocks):
    tokens_here = query_rows.shape[0]
    kv_width = key_rows.shape[1]
    kv_here = kv_width // HEAD_DIM
    groups = query_rows.shape[1] // kv_width
    score_scale = HEAD_DIM ** (-0.5)
    ctx_count = lax.axis_size(CTX)
    ctx_place = lax.axis_index(CTX)
    my_start = ctx_place * tokens_here
    span = REACH * tokens_here
    key_count = span + tokens_here

    own_pair = jnp.concatenate([key_rows, value_rows], axis=1)
    earlier = [from_earlier(own_pair, distance, ctx_count) for distance in range(REACH, 0, -1)]
    pairs_all = jnp.concatenate(earlier + [own_pair], axis=0)
    keys_all = pairs_all[:, :kv_width]
    values_all = pairs_all[:, kv_width:]
    key_heads = keys_all.reshape(key_count, kv_here, HEAD_DIM)
    value_heads = values_all.reshape(key_count, kv_here, HEAD_DIM)

    doc_pad = jnp.concatenate([jnp.full((span,), -1, jnp.int32), doc_ids.astype(jnp.int32)])
    query_pos = my_start + jnp.arange(tokens_here, dtype=jnp.int32)
    key_pos = my_start - span + jnp.arange(key_count, dtype=jnp.int32)
    query_doc = lax.dynamic_slice_in_dim(doc_ids, my_start, tokens_here)
    key_doc = lax.dynamic_slice_in_dim(doc_pad, my_start, key_count)
    query_width = jnp.repeat(
        lax.dynamic_slice_in_dim(window_blocks, my_start // BLOCK, tokens_here // BLOCK), BLOCK
    )
    allowed = (
        (key_pos[None, :] >= 0)
        & (key_pos[None, :] <= query_pos[:, None])
        & (query_doc[:, None] == key_doc[None, :])
        & (query_pos[:, None] // BLOCK - key_pos[None, :] // BLOCK < query_width[:, None])
    )

    query_four = query_rows.reshape(tokens_here, kv_here, groups, HEAD_DIM)
    scores = (
        jnp.einsum("qcgd,kcd->cgqk", query_four, key_heads, preferred_element_type=jnp.float32)
        * score_scale
    )
    masked = jnp.where(allowed, scores, NEG_FILL)
    row_max = jnp.max(masked, axis=-1)
    expo = jnp.where(allowed, jnp.exp(masked - row_max[..., None]), 0.0)
    total = jnp.sum(expo, axis=-1)
    summed = jnp.einsum(
        "cgqk,kcd->qcgd", expo.astype(jnp.bfloat16), value_heads, preferred_element_type=jnp.float32
    )
    attn_four = summed / jnp.transpose(total, (2, 0, 1))[..., None]
    attn = attn_four.reshape(tokens_here, -1).astype(jnp.bfloat16)
    log_sum = row_max + jnp.log(total)
    grad_piece, attn = gathered_over_tp(out_grad, attn)

    weight_part = lax.dot_general(
        grad_piece, attn, (((0,), (0,)), ((), ())), preferred_element_type=jnp.float32
    ).astype(jnp.bfloat16)
    weight_part, attn, grad_piece = lax.optimization_barrier((weight_part, attn, grad_piece))
    weight_sum = lax.psum_scatter(weight_part, CTX[0], scatter_dimension=0, tiled=True)

    out_part = jnp.dot(attn, out_weight, preferred_element_type=jnp.float32)
    layer_out = summed_over_tp(out_part).astype(jnp.bfloat16)
    rest_count = ctx_count // lax.axis_size(CTX[0])
    weight_cols = weight_sum.reshape(rest_count, -1, weight_sum.shape[1])
    weight_cols = lax.all_to_all(weight_cols, CTX[1:], 0, 0, tiled=True)
    weight_sum = jnp.sum(weight_cols.astype(jnp.float32), axis=0).T
    seq_total = ctx_count * tokens_here
    grad_weight = weight_sum * seq_total ** (-0.5)

    d_attn = lax.dot_general(
        grad_piece, out_weight, (((1,), (1,)), ((), ())), preferred_element_type=jnp.float32
    ).astype(jnp.bfloat16)
    grad_four = d_attn.reshape(tokens_here, kv_here, groups, HEAD_DIM)
    delta_rows = jnp.transpose(
        jnp.sum(
            grad_four.astype(jnp.float32)
            * attn.reshape(tokens_here, kv_here, groups, HEAD_DIM).astype(jnp.float32),
            axis=-1,
        ),
        (1, 2, 0),
    )

    probs = jnp.exp(jnp.where(allowed, scores - log_sum[..., None], NEG_FILL))
    d_probs = jnp.einsum(
        "qcgd,kcd->cgqk", grad_four, value_heads, preferred_element_type=jnp.float32
    )
    d_scores = (probs * (d_probs - delta_rows[..., None]) * score_scale).astype(jnp.bfloat16)
    probs_half = probs.astype(jnp.bfloat16)

    def key_side(score_part, prob_part):
        key_part = jnp.einsum(
            "cgqk,qcgd->kcd", score_part, query_four, preferred_element_type=jnp.float32
        )
        value_part = jnp.einsum(
            "cgqk,qcgd->kcd", prob_part, grad_four, preferred_element_type=jnp.float32
        )
        rows = score_part.shape[-1]
        return jnp.concatenate(
            [key_part.reshape(rows, kv_width), value_part.reshape(rows, kv_width)], axis=1
        )

    early_grad = key_side(d_scores[..., :span], probs_half[..., :span]).astype(jnp.bfloat16)
    returned = []
    for distance in range(1, REACH + 1):
        lo = span - distance * tokens_here
        returned.append(to_earlier(early_grad[lo : lo + tokens_here], distance, ctx_count))
    query_grad = jnp.einsum(
        "cgqk,kcd->qcgd", d_scores, key_heads, preferred_element_type=jnp.float32
    )
    pair_grad = key_side(d_scores[..., span:], probs_half[..., span:])
    returned, grad_weight = lax.optimization_barrier((returned, grad_weight))
    for sent in returned:
        pair_grad = pair_grad + sent.astype(jnp.float32)
    key_grad = pair_grad[:, :kv_width]
    value_grad = pair_grad[:, kv_width:]

    grad_queries = query_grad.reshape(tokens_here, -1).astype(jnp.bfloat16)
    grad_keys = key_grad.astype(jnp.bfloat16)
    grad_values = value_grad.astype(jnp.bfloat16)
    return (layer_out, grad_queries, grad_keys, grad_values, grad_weight)


def solution(mesh):
    shape = tuple(size for _, size in CTX_PARTS + TP_PARTS)
    fine = Mesh(np.asarray(mesh.devices).reshape(shape), CTX + TP)
    placed = (
        P(CTX, TP),
        P(CTX, TP),
        P(CTX, TP),
        P(TP, None),
        P(CTX + TP, None),
        P(),
        P(),
    )
    return jax.shard_map(
        on_device,
        mesh=fine,
        in_specs=placed,
        out_specs=(
            P(CTX + TP, None),
            P(CTX, TP),
            P(CTX, TP),
            P(CTX, TP),
            P(TP, CTX),
        ),
        check_vma=False,
    )
```

```python
import jax
import jax.numpy as jnp
import numpy as np
from jax import lax
from jax.sharding import Mesh
from jax.sharding import PartitionSpec as P

HEAD_DIM = 128
BLOCK = 128
REACH = 3
NEG_FILL = -1e30

CTX_PARTS = (("z", 8), ("x", 4), ("y_lo", 2))
TP_PARTS = (("y_hi", 2), ("core", 2))
CTX = tuple(name for name, _ in CTX_PARTS)
TP = tuple(name for name, _ in TP_PARTS)


def from_earlier(block, distance, count):
    route = [(i - distance, i) for i in range(count) if 0 <= i - distance < count]
    return lax.ppermute(block, CTX, route)


def to_earlier(block, distance, count):
    route = [(i, i - distance) for i in range(count) if 0 <= i - distance < count]
    return lax.ppermute(block, CTX, route)


def swapped(block, axis):
    return lax.ppermute(block, axis, [(0, 1), (1, 0)])


def in_order(own, other, place):
    first = jnp.where(place == 0, own, other)
    second = jnp.where(place == 0, other, own)
    return jnp.stack([first, second])


def gathered_over_tp(piece, after):
    high = lax.axis_index(TP[0])
    low = lax.axis_index(TP[1])
    other, after = lax.optimization_barrier((swapped(piece, TP[0]), after))
    by_high = in_order(piece, other, high)
    both = in_order(by_high, swapped(by_high, TP[1]), low)
    return jnp.transpose(both, (1, 0, 2, 3)).reshape(-1, piece.shape[1]), after


def summed_over_tp(part):
    high = lax.axis_index(TP[0])
    low = lax.axis_index(TP[1])
    quarters = part.reshape(2, 2, part.shape[0] // 4, part.shape[1])
    kept = lax.dynamic_index_in_dim(quarters, high, 0, keepdims=False)
    given = lax.dynamic_index_in_dim(quarters, 1 - high, 0, keepdims=False)
    halves = kept + swapped(given.astype(jnp.bfloat16), TP[0]).astype(jnp.float32)
    kept = lax.dynamic_index_in_dim(halves, low, 0, keepdims=False)
    given = lax.dynamic_index_in_dim(halves, 1 - low, 0, keepdims=False)
    return kept + swapped(given.astype(jnp.bfloat16), TP[1]).astype(jnp.float32)


def on_device(query_rows, key_rows, value_rows, out_weight, out_grad, doc_ids, window_blocks):
    tokens_here = query_rows.shape[0]
    kv_width = key_rows.shape[1]
    kv_here = kv_width // HEAD_DIM
    groups = query_rows.shape[1] // kv_width
    score_scale = HEAD_DIM ** (-0.5)
    ctx_count = lax.axis_size(CTX)
    ctx_place = lax.axis_index(CTX)
    my_start = ctx_place * tokens_here
    span = REACH * tokens_here
    key_count = span + tokens_here

    own_pair = jnp.concatenate([key_rows, value_rows], axis=1)
    earlier = [from_earlier(own_pair, distance, ctx_count) for distance in range(REACH, 0, -1)]
    pairs_all = jnp.concatenate(earlier + [own_pair], axis=0)
    keys_all = pairs_all[:, :kv_width]
    values_all = pairs_all[:, kv_width:]
    key_heads = keys_all.reshape(key_count, kv_here, HEAD_DIM)
    value_heads = values_all.reshape(key_count, kv_here, HEAD_DIM)

    doc_pad = jnp.concatenate([jnp.full((span,), -1, jnp.int32), doc_ids.astype(jnp.int32)])
    query_pos = my_start + jnp.arange(tokens_here, dtype=jnp.int32)
    key_pos = my_start - span + jnp.arange(key_count, dtype=jnp.int32)
    query_doc = lax.dynamic_slice_in_dim(doc_ids, my_start, tokens_here)
    key_doc = lax.dynamic_slice_in_dim(doc_pad, my_start, key_count)
    query_width = jnp.repeat(
        lax.dynamic_slice_in_dim(window_blocks, my_start // BLOCK, tokens_here // BLOCK), BLOCK
    )
    allowed = (
        (key_pos[None, :] >= 0)
        & (key_pos[None, :] <= query_pos[:, None])
        & (query_doc[:, None] == key_doc[None, :])
        & (query_pos[:, None] // BLOCK - key_pos[None, :] // BLOCK < query_width[:, None])
    )

    query_four = query_rows.reshape(tokens_here, kv_here, groups, HEAD_DIM)
    scores = (
        jnp.einsum("qcgd,kcd->cgqk", query_four, key_heads, preferred_element_type=jnp.float32)
        * score_scale
    )
    masked = jnp.where(allowed, scores, NEG_FILL)
    row_max = jnp.max(masked, axis=-1)
    expo = jnp.where(allowed, jnp.exp(masked - row_max[..., None]), 0.0)
    total = jnp.sum(expo, axis=-1)
    summed = jnp.einsum(
        "cgqk,kcd->qcgd", expo.astype(jnp.bfloat16), value_heads, preferred_element_type=jnp.float32
    )
    attn_four = summed / jnp.transpose(total, (2, 0, 1))[..., None]
    attn = attn_four.reshape(tokens_here, -1).astype(jnp.bfloat16)
    log_sum = row_max + jnp.log(total)
    grad_piece, attn = gathered_over_tp(out_grad, attn)

    weight_part = lax.dot_general(
        grad_piece, attn, (((0,), (0,)), ((), ())), preferred_element_type=jnp.float32
    ).astype(jnp.bfloat16)
    weight_part, attn, grad_piece = lax.optimization_barrier((weight_part, attn, grad_piece))
    weight_sum = lax.psum_scatter(weight_part, CTX[0], scatter_dimension=0, tiled=True)

    out_part = jnp.dot(attn, out_weight, preferred_element_type=jnp.float32)
    layer_out = summed_over_tp(out_part).astype(jnp.bfloat16)
    rest_count = ctx_count // lax.axis_size(CTX[0])
    weight_cols = weight_sum.reshape(rest_count, -1, weight_sum.shape[1])
    weight_cols = lax.all_to_all(weight_cols, CTX[1:], 0, 0, tiled=True)
    weight_sum = jnp.sum(weight_cols.astype(jnp.float32), axis=0).T
    seq_total = ctx_count * tokens_here
    grad_weight = weight_sum * seq_total ** (-0.5)

    d_attn = lax.dot_general(
        grad_piece, out_weight, (((1,), (1,)), ((), ())), preferred_element_type=jnp.float32
    ).astype(jnp.bfloat16)
    grad_four = d_attn.reshape(tokens_here, kv_here, groups, HEAD_DIM)
    delta_rows = jnp.transpose(
        jnp.sum(
            grad_four.astype(jnp.float32)
            * attn.reshape(tokens_here, kv_here, groups, HEAD_DIM).astype(jnp.float32),
            axis=-1,
        ),
        (1, 2, 0),
    )

    probs = jnp.exp(jnp.where(allowed, scores - log_sum[..., None], NEG_FILL))
    d_probs = jnp.einsum(
        "qcgd,kcd->cgqk", grad_four, value_heads, preferred_element_type=jnp.float32
    )
    d_scores = (probs * (d_probs - delta_rows[..., None]) * score_scale).astype(jnp.bfloat16)
    probs_half = probs.astype(jnp.bfloat16)

    def key_side(score_part, prob_part):
        key_part = jnp.einsum(
            "cgqk,qcgd->kcd", score_part, query_four, preferred_element_type=jnp.float32
        )
        value_part = jnp.einsum(
            "cgqk,qcgd->kcd", prob_part, grad_four, preferred_element_type=jnp.float32
        )
        rows = score_part.shape[-1]
        return jnp.concatenate(
            [key_part.reshape(rows, kv_width), value_part.reshape(rows, kv_width)], axis=1
        )

    early_grad = key_side(d_scores[..., :span], probs_half[..., :span]).astype(jnp.bfloat16)
    early_grad, d_scores, probs_half = lax.optimization_barrier((early_grad, d_scores, probs_half))
    returned = []
    for distance in range(1, REACH + 1):
        lo = span - distance * tokens_here
        returned.append(to_earlier(early_grad[lo : lo + tokens_here], distance, ctx_count))
    query_grad = jnp.einsum(
        "cgqk,kcd->qcgd", d_scores, key_heads, preferred_element_type=jnp.float32
    )
    pair_grad = key_side(d_scores[..., span:], probs_half[..., span:])
    returned, grad_weight = lax.optimization_barrier((returned, grad_weight))
    for sent in returned:
        pair_grad = pair_grad + sent.astype(jnp.float32)
    key_grad = pair_grad[:, :kv_width]
    value_grad = pair_grad[:, kv_width:]

    grad_queries = query_grad.reshape(tokens_here, -1).astype(jnp.bfloat16)
    grad_keys = key_grad.astype(jnp.bfloat16)
    grad_values = value_grad.astype(jnp.bfloat16)
    return (layer_out, grad_queries, grad_keys, grad_values, grad_weight)


def solution(mesh):
    shape = tuple(size for _, size in CTX_PARTS + TP_PARTS)
    fine = Mesh(np.asarray(mesh.devices).reshape(shape), CTX + TP)
    placed = (
        P(CTX, TP),
        P(CTX, TP),
        P(CTX, TP),
        P(TP, None),
        P(CTX + TP, None),
        P(),
        P(),
    )
    return jax.shard_map(
        on_device,
        mesh=fine,
        in_specs=placed,
        out_specs=(
            P(CTX + TP, None),
            P(CTX, TP),
            P(CTX, TP),
            P(CTX, TP),
            P(TP, CTX),
        ),
        check_vma=False,
    )
```
